512 devices in a mesh: blk: 32 (over z_hi, x, core), head: 16 (over y, z_lo).
Axes of the slice: x: 4, y: 8, z: 8 (z_hi: 4, z_lo: 2; z = z_hi * 2 + z_lo), core: 2. Of those that a mesh axis runs over, the one named last changes fastest.
Arguments:
- query_rows: bfloat16 [65536, 1024], P(('blk', 'head')), may hold values from -6 to 6
- key_rows: bfloat16 [65536, 1024], P(('blk', 'head')), may hold values from -6 to 6
- value_rows: bfloat16 [65536, 1024], P(('blk', 'head')), may hold values from -6 to 6
- out_grad: bfloat16 [65536, 1024], P(('blk', 'head')), may hold values from -6 to 6
- neighbour_blocks: int32 [128, 2], replicated, may hold values from 0 to 3
Outputs:
- attended: bfloat16 [65536, 1024], P(('blk', 'head'))
- query_grad: bfloat16 [65536, 1024], P(('blk', 'head'))
- key_grad: bfloat16 [65536, 1024], P(('blk', 'head'))
- value_grad: bfloat16 [65536, 1024], P(('blk', 'head'))
The draws below stay inside these ranges and needn't reach their ends.
Inputs may be any that keep to these rules, and one draw needn't show every extreme that they name: neighbour_blocks[g, 0] and neighbour_blocks[g, 1] number a block within the previous and the next segment, counted from that segment's first block.
All inputs are finite; a program needn't handle non-finite values.
Results may differ from the reference program's by a relative error of at most 0.012.
The reference program's roundings to bfloat16 on the way count: a program that leaves them out, or rounds other values in their place, can miss the bound.
Values may be sent and summed in bfloat16 or wider, within the bound.
No kernel may reach another device: no remote copies, remote signals or barrier semaphores. Data moves between devices by JAX's collectives and lax.ppermute only.
A program may use at most 64 MiB of HBM per device.

```python
import jax
import jax.numpy as jnp
from jax import lax

HEADS = 16
HEAD_DIM = 64
WIDTH = 1024
BLOCK = 512
SEQ = 65536
SEG_BLOCKS = 4
ALL_BLOCKS = 128
N_BLK = 32


def drawn_rows(key):
    folded = jax.random.fold_in(key, 4217)
    pieces = jax.random.split(folded, 2)
    full_shape = (SEQ, WIDTH)
    queries = jnp.clip(jax.random.normal(pieces[0], full_shape, jnp.float32), -6.0, 6.0)
    keyset = jnp.clip(jax.random.normal(pieces[1], full_shape, jnp.float32), -6.0, 6.0)
    return (queries, keyset)


def draw_query_rows(key, part):
    return drawn_rows(key)[0].astype(jnp.bfloat16)


def draw_key_rows(key, part):
    return drawn_rows(key)[1].astype(jnp.bfloat16)


def touch_ends(drawn, stream_key, smallest, largest):
    index_at = [jax.random.randint(jax.random.fold_in(stream_key, axis), (), 0, length) for axis, length in enumerate(drawn.shape)]
    longest = drawn.shape.index(max(drawn.shape))
    beside = index_at[:longest] + [(index_at[longest] + 1) % drawn.shape[longest]] + index_at[longest + 1:]
    return drawn.at[tuple(index_at)].set(smallest).at[tuple(beside)].set(largest)


def level_of(key, extent, shards, least, largest):
    level = 1.0
    for position, shards_of in shards:
        heights = jax.random.uniform(jax.random.fold_in(jax.random.fold_in(key, 6), position), (shards_of,), jnp.float32, least / len(shards), largest / len(shards))
        level = level * jnp.repeat(jnp.exp(heights), extent[position] // shards_of).reshape((-1,) + (1,) * (len(extent) - 1 - position))
    return level


def bell_draw(stream_key, shape, spread, most, cuts=(), held_as=jnp.bfloat16):
    values = spread * jax.random.normal(stream_key, shape, jnp.float32)
    if cuts:
        values = values * level_of(stream_key, shape, cuts, -0.22, 0.18)
    return jnp.clip(values, -most, most).astype(held_as)


def setup_inputs(seed: int = 0) -> dict:
    key_of = jax.random.split(jax.random.key(seed), 6)
    return {
        "query_rows": draw_query_rows(jax.random.fold_in(key_of[5], 71), 0),
        "key_rows": draw_key_rows(jax.random.fold_in(key_of[5], 71), 0),
        "value_rows": bell_draw(key_of[2], (SEQ, WIDTH), 1.0, 6.0, ((0, 512),)),
        "out_grad": bell_draw(key_of[3], (SEQ, WIDTH), 1.0, 6.0, ((0, 512),)),
        "neighbour_blocks": touch_ends(jax.random.randint(key_of[4], (ALL_BLOCKS, 2), 0, SEG_BLOCKS), jax.random.fold_in(key_of[4], 1), 0, SEG_BLOCKS - 1).astype(jnp.int32),
    }


def settle(source):
    return lax.optimization_barrier(source.astype(jnp.bfloat16)).astype(jnp.float32)


def reference(query_rows, key_rows, value_rows, out_grad, neighbour_blocks):
    factor = HEAD_DIM ** -0.5
    block_shape = (ALL_BLOCKS, BLOCK, HEADS, HEAD_DIM)
    query_all = query_rows.astype(jnp.float32).reshape(block_shape)
    key_all = key_rows.astype(jnp.float32).reshape(block_shape)
    value_all = value_rows.astype(jnp.float32).reshape(block_shape)
    grad_all = out_grad.astype(jnp.float32).reshape(block_shape)
    block_index = jnp.arange(ALL_BLOCKS, dtype=jnp.int32)
    segment = block_index // SEG_BLOCKS
    left_ids = ((segment - 1) % N_BLK) * SEG_BLOCKS + neighbour_blocks[:, 0].astype(jnp.int32)
    right_ids = ((segment + 1) % N_BLK) * SEG_BLOCKS + neighbour_blocks[:, 1].astype(jnp.int32)
    block_ids = jnp.stack([block_index, left_ids, right_ids], axis=1).astype(jnp.int32)
    positions = jnp.arange(BLOCK, dtype=jnp.int32)
    allowed = jnp.concatenate([positions[None, :] <= positions[:, None], jnp.ones((BLOCK, 2 * BLOCK), dtype=bool)], axis=1)

    def key_set(source, chosen):
        return source[chosen].reshape(3 * BLOCK, HEADS, HEAD_DIM)

    def forward_one(number):
        chosen = block_ids[number]
        key_block = key_set(key_all, chosen)
        value_block = key_set(value_all, chosen)
        scores = jnp.einsum("qhd,khd->hqk", query_all[number], key_block) * factor
        scores = jnp.where(allowed[None], scores, -jnp.inf)
        highest = jnp.max(scores, axis=2, keepdims=True)
        log_total = highest + jnp.log(jnp.sum(jnp.exp(scores - highest), axis=2, keepdims=True))
        weights = settle(jnp.exp(scores - log_total))
        attended = jnp.einsum("hqk,khd->qhd", weights, value_block).astype(jnp.bfloat16)
        return attended, log_total[:, :, 0]

    out_blocks, log_totals = lax.map(forward_one, block_index)
    row_deltas = jnp.sum(grad_all * out_blocks.astype(jnp.float32), axis=3).transpose(0, 2, 1)

    def backward_one(carry, number):
        key_acc, value_acc = carry
        chosen = block_ids[number]
        key_block = key_set(key_all, chosen)
        value_block = key_set(value_all, chosen)
        scores = jnp.einsum("qhd,khd->hqk", query_all[number], key_block) * factor
        weights = jnp.where(allowed[None], jnp.exp(scores - log_totals[number][:, :, None]), 0.0)
        weight_grad = jnp.einsum("qhd,khd->hqk", grad_all[number], value_block)
        score_grad = settle(weights * (weight_grad - row_deltas[number][:, :, None]))
        query_part = jnp.einsum("hqk,khd->qhd", score_grad, key_block) * factor
        key_part = jnp.einsum("hqk,qhd->khd", score_grad, query_all[number]) * factor
        value_part = jnp.einsum("hqk,qhd->khd", settle(weights), grad_all[number])
        key_acc = key_acc.at[chosen].add(key_part.reshape(3, BLOCK, HEADS, HEAD_DIM))
        value_acc = value_acc.at[chosen].add(value_part.reshape(3, BLOCK, HEADS, HEAD_DIM))
        return (key_acc, value_acc), query_part

    zeros_start = jnp.zeros(block_shape, jnp.float32)
    (key_acc, value_acc), query_parts = lax.scan(backward_one, (zeros_start, zeros_start), block_index)
    attended = out_blocks.reshape(SEQ, WIDTH)
    query_grad = query_parts.reshape(SEQ, WIDTH).astype(jnp.bfloat16)
    key_grad = key_acc.reshape(SEQ, WIDTH).astype(jnp.bfloat16)
    value_grad = value_acc.reshape(SEQ, WIDTH).astype(jnp.bfloat16)
    return (attended, query_grad, key_grad, value_grad)
```

```python
import jax
import jax.numpy as jnp
from jax import lax
from jax.sharding import PartitionSpec as P

HEAD_DIM = 64
BLOCK = 512


def extended(x, sides, width):
    for axis, dim in sides:
        count, length = (lax.axis_size(axis), x.shape[dim])
        up = [(i, (i + 1) % count) for i in range(count)]
        down = [(j, i) for i, j in up]
        last = lax.slice_in_dim(x, length - width, length, axis=dim)
        leading = lax.slice_in_dim(x, 0, width, axis=dim)
        before = lax.ppermute(last, axis, up)
        after = lax.ppermute(leading, axis, down)
        x = jnp.concatenate([before, x, after], axis=dim)
    return x


def shortened(x):
    return jax.tree.map(lambda a: a.astype(jnp.bfloat16) if a.dtype == jnp.float32 else a, x)


def from_behind(value, axis, steps):
    count = lax.axis_size(axis)
    pairs = [(source, (source + steps) % count) for source in range(count)]
    return lax.ppermute(value, axis, pairs)


def scaled_scores(query_block, key_block):
    product = jnp.einsum("qgd,kgd->gqk", query_block, key_block, preferred_element_type=jnp.float32)
    return product * HEAD_DIM ** (-0.5)


def forward_block(query_block, key_block, value_block, allowed):
    scores = jnp.where(allowed[None], scaled_scores(query_block, key_block), -jnp.inf)
    highest = jnp.max(scores, axis=2, keepdims=True)
    log_total = highest + jnp.log(jnp.sum(jnp.exp(scores - highest), axis=2, keepdims=True))
    weights = jnp.exp(scores - log_total).astype(jnp.bfloat16)
    attended = jnp.einsum("gqk,kgd->qgd", weights, value_block, preferred_element_type=jnp.float32)
    return (attended.astype(jnp.bfloat16), log_total[:, :, 0])


def gradient_block(query_block, grad_block, log_total, row_delta, key_block, value_block, allowed):
    weights = jnp.exp(scaled_scores(query_block, key_block) - log_total[:, :, None])
    weights = jnp.where(allowed[None], weights, 0.0)
    weight_grad = jnp.einsum(
        "qgd,kgd->gqk", grad_block, value_block, preferred_element_type=jnp.float32
    )
    score_grad = (weights * (weight_grad - row_delta[:, :, None])).astype(jnp.bfloat16)
    factor = HEAD_DIM ** (-0.5)
    results = []
    results.append(
        jnp.einsum("gqk,kgd->qgd", score_grad, key_block, preferred_element_type=jnp.float32)
        * factor
    )
    key_part = (
        jnp.einsum("gqk,qgd->kgd", score_grad, query_block, preferred_element_type=jnp.float32)
        * factor
    )
    value_part = jnp.einsum(
        "gqk,qgd->kgd", weights.astype(jnp.bfloat16), grad_block, preferred_element_type=jnp.float32
    )
    results.append(jnp.stack([key_part, value_part], axis=1))
    return tuple(results)


def to_heads(arrays):
    count = lax.axis_size("head")
    rows, width = arrays[0].shape
    stacked = jnp.stack(arrays).reshape(len(arrays), rows, count, width // count)
    stacked = stacked.transpose(2, 0, 1, 3)
    moved = lax.all_to_all(stacked, "head", split_axis=0, concat_axis=0, tiled=True)
    moved = moved.transpose(1, 0, 2, 3).reshape(len(arrays), count * rows, width // count)
    return [moved[i] for i in range(len(arrays))]


def to_rows(arrays):
    count = lax.axis_size("head")
    rows, width = arrays[0].shape
    stacked = jnp.stack(arrays).reshape(len(arrays), count, rows // count, width)
    stacked = stacked.transpose(1, 0, 2, 3)
    moved = lax.all_to_all(stacked, "head", split_axis=0, concat_axis=0, tiled=True)
    moved = moved.transpose(1, 2, 0, 3).reshape(len(arrays), rows // count, count * width)
    return [moved[i] for i in range(len(arrays))]


def shards(query_rows, key_rows, value_rows, out_grad, neighbour_blocks):
    query_heads, key_heads, value_heads, grad_heads = to_heads(
        [query_rows, key_rows, value_rows, out_grad]
    )
    row_count = query_heads.shape[0]
    feature_count = query_heads.shape[1]
    head_count = feature_count // HEAD_DIM
    block_count = row_count // BLOCK
    cycle_size = lax.axis_size("blk")
    cycle_place = lax.axis_index("blk")
    block_range = jnp.arange(block_count, dtype=jnp.int32)

    def split_blocks(source):
        return source.reshape(block_count, BLOCK, head_count, HEAD_DIM)

    def split_pairs(source):
        return source.reshape(block_count, BLOCK, 2, head_count, HEAD_DIM)

    def picks_of(column):
        first_row = cycle_place % cycle_size * block_count
        return lax.dynamic_slice_in_dim(neighbour_blocks[:, column], first_row, block_count, 0)

    def route(picked, pieces):
        onehot = (picked[None, :] == block_range[:, None]).astype(jnp.float32)
        summed = jnp.dot(onehot, pieces.reshape(block_count, -1), precision=lax.Precision.HIGHEST)
        return summed.reshape(row_count, -1)

    paired = jnp.concatenate([key_heads, value_heads], axis=1)
    key_window = extended(paired, (("blk", 0),), row_count)
    own_pairs = split_pairs(paired)
    left_pairs = split_pairs(key_window[:row_count])
    right_pairs = split_pairs(key_window[2 * row_count :])
    left_picks = picks_of(0)
    right_picks = picks_of(1)
    positions = jnp.arange(BLOCK, dtype=jnp.int32)
    causal = positions[None, :] <= positions[:, None]
    allowed = jnp.concatenate([causal, jnp.ones((BLOCK, 2 * BLOCK), dtype=bool)], axis=1)
    query_blocks = split_blocks(query_heads)
    grad_blocks = split_blocks(grad_heads)

    def key_set(number):
        stacked = jnp.concatenate(
            [own_pairs[number], left_pairs[left_picks[number]], right_pairs[right_picks[number]]],
            axis=0,
        )
        return (stacked[:, 0], stacked[:, 1])

    def forward_one(number):
        key_block, value_block = key_set(number)
        return forward_block(query_blocks[number], key_block, value_block, allowed)

    out_blocks, log_totals = lax.map(forward_one, block_range)
    attended_heads = out_blocks.reshape(row_count, feature_count)
    row_deltas = jnp.sum(
        grad_blocks.astype(jnp.float32) * out_blocks.astype(jnp.float32), axis=3
    ).transpose(0, 2, 1)

    def backward_one(number):
        key_block, value_block = key_set(number)
        return gradient_block(
            query_blocks[number],
            grad_blocks[number],
            log_totals[number],
            row_deltas[number],
            key_block,
            value_block,
            allowed,
        )

    query_parts, key_parts = lax.map(backward_one, block_range)
    own_grads = key_parts[:, :BLOCK].reshape(row_count, -1)
    to_left = route(left_picks, key_parts[:, BLOCK : 2 * BLOCK])
    to_right = route(right_picks, key_parts[:, 2 * BLOCK :])
    from_right = from_behind(shortened(to_left), "blk", -1).astype(to_left.dtype)
    from_left = from_behind(shortened(to_right), "blk", 1).astype(to_right.dtype)
    key_total = own_grads + from_right + from_left
    query_grad_heads = query_parts.reshape(row_count, feature_count).astype(jnp.bfloat16)
    split_total = key_total.reshape(row_count, 2, feature_count)
    key_grad_heads = split_total[:, 0].astype(jnp.bfloat16)
    value_grad_heads = split_total[:, 1].astype(jnp.bfloat16)
    attended, query_grad, key_grad, value_grad = to_rows(
        [attended_heads.astype(jnp.bfloat16), query_grad_heads, key_grad_heads, value_grad_heads]
    )
    return (attended, query_grad, key_grad, value_grad)


def solution(mesh):
    in_specs = (
        P(("blk", "head"), None),
        P(("blk", "head"), None),
        P(("blk", "head"), None),
        P(("blk", "head"), None),
        P(),
    )
    out_specs = (
        P(("blk", "head"), None),
        P(("blk", "head"), None),
        P(("blk", "head"), None),
        P(("blk", "head"), None),
    )
    return jax.shard_map(shards, mesh=mesh, in_specs=in_specs, out_specs=out_specs, check_vma=False)
```

```python
import jax
import jax.numpy as jnp
from jax import lax
from jax.experimental import pallas as pl
from jax.experimental.pallas import tpu as pltpu
from jax.sharding import PartitionSpec as P

HEAD_DIM = 64
BLOCK = 512
INTERPRET = False


def to_heads(arrays):
    count = lax.axis_size("head")
    rows, width = arrays[0].shape
    stacked = jnp.stack(arrays).reshape(len(arrays), rows, count, width // count)
    stacked = stacked.transpose(2, 0, 1, 3)
    moved = lax.all_to_all(stacked, "head", split_axis=0, concat_axis=0, tiled=True)
    return moved.transpose(1, 0, 2, 3).reshape(len(arrays), count * rows, width // count)


def to_rows(stacked):
    count = lax.axis_size("head")
    parts, rows, width = stacked.shape
    stacked = stacked.reshape(parts, count, rows // count, width).transpose(1, 0, 2, 3)
    moved = lax.all_to_all(stacked, "head", split_axis=0, concat_axis=0, tiled=True)
    moved = moved.transpose(1, 2, 0, 3).reshape(parts, rows // count, count * width)
    return [moved[i] for i in range(parts)]


def from_behind(value, axis, steps):
    count = lax.axis_size(axis)
    pairs = [(source, (source + steps) % count) for source in range(count)]
    return lax.ppermute(value, axis, pairs)


def attention_kernel(picks_ref, own_ref, left_ref, right_ref, out_ref, own_grad_ref, left_ref_acc, right_ref_acc):
    number = pl.program_id(0)
    scale = HEAD_DIM ** (-0.5)
    f32 = jnp.float32

    @pl.when(number == 0)
    def _():
        left_ref_acc[...] = jnp.zeros(left_ref_acc.shape, f32)
        right_ref_acc[...] = jnp.zeros(right_ref_acc.shape, f32)

    query = own_ref[0, 0]
    grad = own_ref[3, 0]
    keys = (own_ref[1, 0], left_ref[0, 0], right_ref[0, 0])
    values = (own_ref[2, 0], left_ref[1, 0], right_ref[1, 0])

    def nt(a, b):
        return lax.dot_general(a, b, (((1,), (1,)), ((), ())), preferred_element_type=f32)

    def nn(a, b):
        return lax.dot_general(a, b, (((1,), (0,)), ((), ())), preferred_element_type=f32)

    def tn(a, b):
        return lax.dot_general(a, b, (((0,), (0,)), ((), ())), preferred_element_type=f32)

    scores = [nt(query, key) * scale for key in keys]
    row = lax.broadcasted_iota(jnp.int32, scores[0].shape, 0)
    col = lax.broadcasted_iota(jnp.int32, scores[0].shape, 1)
    scores[0] = jnp.where(col <= row, scores[0], -jnp.inf)
    highest = jnp.max(scores[0], axis=1, keepdims=True)
    for part in scores[1:]:
        highest = jnp.maximum(highest, jnp.max(part, axis=1, keepdims=True))
    total = sum(jnp.sum(jnp.exp(part - highest), axis=1, keepdims=True) for part in scores)
    log_total = highest + jnp.log(total)
    weights = [jnp.exp(part - log_total) for part in scores]
    weights_bf = [w.astype(jnp.bfloat16) for w in weights]
    attended = sum(nn(w, v) for w, v in zip(weights_bf, values)).astype(jnp.bfloat16)
    row_delta = jnp.sum(grad.astype(f32) * attended.astype(f32), axis=1, keepdims=True)
    score_grads = [
        (w * (nt(grad, v) - row_delta)).astype(jnp.bfloat16) for w, v in zip(weights, values)
    ]
    query_grad = sum(nn(d, k) for d, k in zip(score_grads, keys)) * scale
    out_ref[0, 0] = attended
    out_ref[1, 0] = query_grad.astype(jnp.bfloat16)
    key_parts = [tn(d, query) * scale for d in score_grads]
    value_parts = [tn(w, grad) for w in weights_bf]
    own_grad_ref[0, 0] = key_parts[0]
    own_grad_ref[1, 0] = value_parts[0]
    left_pick = picks_ref[0, number]
    right_pick = picks_ref[1, number]
    left_ref_acc[0, left_pick] += key_parts[1]
    left_ref_acc[1, left_pick] += value_parts[1]
    right_ref_acc[0, right_pick] += key_parts[2]
    right_ref_acc[1, right_pick] += value_parts[2]


def attention(picks, own, left, right):
    arrays, block_count, block, dim = own.shape
    own_spec = pl.BlockSpec((arrays, 1, block, dim), lambda n, p: (0, n, 0, 0))
    left_spec = pl.BlockSpec((2, 1, block, dim), lambda n, p: (0, p[0, n], 0, 0))
    right_spec = pl.BlockSpec((2, 1, block, dim), lambda n, p: (0, p[1, n], 0, 0))
    pair_spec = pl.BlockSpec((2, 1, block, dim), lambda n, p: (0, n, 0, 0))
    whole_spec = pl.BlockSpec((2, block_count, block, dim), lambda n, p: (0, 0, 0, 0))
    pair_shape = (2, block_count, block, dim)
    return pl.pallas_call(
        attention_kernel,
        grid_spec=pltpu.PrefetchScalarGridSpec(
            num_scalar_prefetch=1,
            grid=(block_count,),
            in_specs=[own_spec, left_spec, right_spec],
            out_specs=[pair_spec, pair_spec, whole_spec, whole_spec],
        ),
        out_shape=[
            jax.ShapeDtypeStruct(pair_shape, jnp.bfloat16),
            jax.ShapeDtypeStruct(pair_shape, jnp.float32),
            jax.ShapeDtypeStruct(pair_shape, jnp.float32),
            jax.ShapeDtypeStruct(pair_shape, jnp.float32),
        ],
        compiler_params=pltpu.CompilerParams(dimension_semantics=("arbitrary",)),
        interpret=INTERPRET,
    )(picks, own, left, right)


def shards(query_rows, key_rows, value_rows, out_grad, neighbour_blocks):
    heads = to_heads([query_rows, key_rows, value_rows, out_grad])
    arrays, row_count, dim = heads.shape
    block_count = row_count // BLOCK
    own = heads.reshape(arrays, block_count, BLOCK, dim)
    cycle_place = lax.axis_index("blk")
    first_row = cycle_place * block_count
    picks = jnp.stack(
        [lax.dynamic_slice_in_dim(neighbour_blocks[:, c], first_row, block_count, 0) for c in range(2)]
    )
    picks = jnp.clip(picks, 0, block_count - 1).astype(jnp.int32)
    pairs = own[1:3]
    left = from_behind(pairs, "blk", 1)
    right = from_behind(pairs, "blk", -1)
    out_pair, own_grads, to_left, to_right = attention(picks, own, left, right)
    from_right = from_behind(to_left.astype(jnp.bfloat16), "blk", -1).astype(jnp.float32)
    from_left = from_behind(to_right.astype(jnp.bfloat16), "blk", 1).astype(jnp.float32)
    kv_grads = (own_grads + from_right + from_left).astype(jnp.bfloat16)
    stacked = jnp.concatenate([out_pair, kv_grads], axis=0).reshape(4, row_count, dim)
    attended, query_grad, key_grad, value_grad = to_rows(stacked)
    return (attended, query_grad, key_grad, value_grad)


def solution(mesh):
    in_specs = (
        P(("blk", "head"), None),
        P(("blk", "head"), None),
        P(("blk", "head"), None),
        P(("blk", "head"), None),
        P(),
    )
    out_specs = (
        P(("blk", "head"), None),
        P(("blk", "head"), None),
        P(("blk", "head"), None),
        P(("blk", "head"), None),
    )
    return jax.shard_map(shards, mesh=mesh, in_specs=in_specs, out_specs=out_specs, check_vma=False)
```

```python
import jax
import jax.numpy as jnp
from jax import lax
from jax.experimental import pallas as pl
from jax.experimental.pallas import tpu as pltpu
from jax.sharding import PartitionSpec as P

HEAD_DIM = 64
BLOCK = 512
INTERPRET = False


def to_heads(arrays):
    count = lax.axis_size("head")
    rows, width = arrays[0].shape
    stacked = jnp.stack(arrays).reshape(len(arrays), rows, count, width // count)
    stacked = stacked.transpose(2, 0, 1, 3)
    moved = lax.all_to_all(stacked, "head", split_axis=0, concat_axis=0, tiled=True)
    return moved.transpose(1, 0, 2, 3).reshape(len(arrays), count * rows, width // count)


def to_rows(stacked):
    count = lax.axis_size("head")
    parts, rows, width = stacked.shape
    stacked = stacked.reshape(parts, count, rows // count, width).transpose(1, 0, 2, 3)
    moved = lax.all_to_all(stacked, "head", split_axis=0, concat_axis=0, tiled=True)
    moved = moved.transpose(1, 2, 0, 3).reshape(parts, rows // count, count * width)
    return [moved[i] for i in range(parts)]


def from_behind(value, axis, steps):
    count = lax.axis_size(axis)
    pairs = [(source, (source + steps) % count) for source in range(count)]
    return lax.ppermute(value, axis, pairs)


def attention_kernel(picks_ref, qd_ref, kv_ref, left_ref, right_ref, out_ref, own_grad_ref, left_ref_acc, right_ref_acc):
    number = pl.program_id(0)
    scale = HEAD_DIM ** (-0.5)
    f32 = jnp.float32

    @pl.when(number == 0)
    def _():
        left_ref_acc[...] = jnp.zeros(left_ref_acc.shape, f32)
        right_ref_acc[...] = jnp.zeros(right_ref_acc.shape, f32)

    query = qd_ref[0, 0]
    grad = qd_ref[1, 0]
    keys = (kv_ref[0, 0], left_ref[0, 0], right_ref[0, 0])
    values = (kv_ref[1, 0], left_ref[1, 0], right_ref[1, 0])

    def nt(a, b):
        return lax.dot_general(a, b, (((1,), (1,)), ((), ())), preferred_element_type=f32)

    def nn(a, b):
        return lax.dot_general(a, b, (((1,), (0,)), ((), ())), preferred_element_type=f32)

    def tn(a, b):
        return lax.dot_general(a, b, (((0,), (0,)), ((), ())), preferred_element_type=f32)

    scores = [nt(query, key) * scale for key in keys]
    row = lax.broadcasted_iota(jnp.int32, scores[0].shape, 0)
    col = lax.broadcasted_iota(jnp.int32, scores[0].shape, 1)
    scores[0] = jnp.where(col <= row, scores[0], -jnp.inf)
    highest = jnp.max(scores[0], axis=1, keepdims=True)
    for part in scores[1:]:
        highest = jnp.maximum(highest, jnp.max(part, axis=1, keepdims=True))
    total = sum(jnp.sum(jnp.exp(part - highest), axis=1, keepdims=True) for part in scores)
    log_total = highest + jnp.log(total)
    weights = [jnp.exp(part - log_total) for part in scores]
    weights_bf = [w.astype(jnp.bfloat16) for w in weights]
    attended = sum(nn(w, v) for w, v in zip(weights_bf, values)).astype(jnp.bfloat16)
    row_delta = jnp.sum(grad.astype(f32) * attended.astype(f32), axis=1, keepdims=True)
    score_grads = [
        (w * (nt(grad, v) - row_delta)).astype(jnp.bfloat16) for w, v in zip(weights, values)
    ]
    query_grad = sum(nn(d, k) for d, k in zip(score_grads, keys)) * scale
    out_ref[0, 0] = attended
    out_ref[1, 0] = query_grad.astype(jnp.bfloat16)
    key_parts = [tn(d, query) * scale for d in score_grads]
    value_parts = [tn(w, grad) for w in weights_bf]
    own_grad_ref[0, 0] = key_parts[0]
    own_grad_ref[1, 0] = value_parts[0]
    left_pick = picks_ref[0, number]
    right_pick = picks_ref[1, number]
    left_ref_acc[0, left_pick] += key_parts[1]
    left_ref_acc[1, left_pick] += value_parts[1]
    right_ref_acc[0, right_pick] += key_parts[2]
    right_ref_acc[1, right_pick] += value_parts[2]


def attention(picks, qd, kv, left, right):
    arrays, block_count, block, dim = kv.shape
    left_spec = pl.BlockSpec((2, 1, block, dim), lambda n, p: (0, p[0, n], 0, 0))
    right_spec = pl.BlockSpec((2, 1, block, dim), lambda n, p: (0, p[1, n], 0, 0))
    pair_spec = pl.BlockSpec((2, 1, block, dim), lambda n, p: (0, n, 0, 0))
    whole_spec = pl.BlockSpec((2, block_count, block, dim), lambda n, p: (0, 0, 0, 0))
    pair_shape = (2, block_count, block, dim)
    return pl.pallas_call(
        attention_kernel,
        grid_spec=pltpu.PrefetchScalarGridSpec(
            num_scalar_prefetch=1,
            grid=(block_count,),
            in_specs=[pair_spec, pair_spec, left_spec, right_spec],
            out_specs=[pair_spec, pair_spec, whole_spec, whole_spec],
        ),
        out_shape=[
            jax.ShapeDtypeStruct(pair_shape, jnp.bfloat16),
            jax.ShapeDtypeStruct(pair_shape, jnp.float32),
            jax.ShapeDtypeStruct(pair_shape, jnp.float32),
            jax.ShapeDtypeStruct(pair_shape, jnp.float32),
        ],
        compiler_params=pltpu.CompilerParams(dimension_semantics=("arbitrary",)),
        interpret=INTERPRET,
    )(picks, qd, kv, left, right)


def shards(query_rows, key_rows, value_rows, out_grad, neighbour_blocks):
    kv_heads = to_heads([key_rows, value_rows])
    arrays, row_count, dim = kv_heads.shape
    block_count = row_count // BLOCK
    pairs = kv_heads.reshape(arrays, block_count, BLOCK, dim)
    left = from_behind(pairs, "blk", 1)
    right = from_behind(pairs, "blk", -1)
    qd = to_heads([query_rows, out_grad]).reshape(arrays, block_count, BLOCK, dim)
    cycle_place = lax.axis_index("blk")
    first_row = cycle_place * block_count
    picks = jnp.stack(
        [lax.dynamic_slice_in_dim(neighbour_blocks[:, c], first_row, block_count, 0) for c in range(2)]
    )
    picks = jnp.clip(picks, 0, block_count - 1).astype(jnp.int32)
    out_pair, own_grads, to_left, to_right = attention(picks, qd, pairs, left, right)
    from_right = from_behind(to_left.astype(jnp.bfloat16), "blk", -1).astype(jnp.float32)
    from_left = from_behind(to_right.astype(jnp.bfloat16), "blk", 1).astype(jnp.float32)
    attended, query_grad = to_rows(out_pair.reshape(2, row_count, dim))
    kv_grads = (own_grads + from_right + from_left).astype(jnp.bfloat16)
    key_grad, value_grad = to_rows(kv_grads.reshape(2, row_count, dim))
    return (attended, query_grad, key_grad, value_grad)


def solution(mesh):
    in_specs = (
        P(("blk", "head"), None),
        P(("blk", "head"), None),
        P(("blk", "head"), None),
        P(("blk", "head"), None),
        P(),
    )
    out_specs = (
        P(("blk", "head"), None),
        P(("blk", "head"), None),
        P(("blk", "head"), None),
        P(("blk", "head"), None),
    )
    return jax.shard_map(shards, mesh=mesh, in_specs=in_specs, out_specs=out_specs, check_vma=False)
```

```python
import jax
import jax.numpy as jnp
from jax import lax
from jax.experimental import pallas as pl
from jax.experimental.pallas import tpu as pltpu
from jax.sharding import PartitionSpec as P

HEAD_DIM = 64
BLOCK = 512
INTERPRET = False


def to_heads(first, second):
    count = lax.axis_size("head")
    rows, width = first.shape
    split = [a.reshape(rows, count, width // count) for a in (first, second)]
    packed = jnp.concatenate(split, axis=2)
    moved = lax.all_to_all(packed, "head", split_axis=1, concat_axis=0, tiled=True)
    return moved.reshape(count * rows, 2 * width // count)


def to_rows(packed):
    count = lax.axis_size("head")
    rows, width = packed.shape
    moved = lax.all_to_all(packed, "head", split_axis=0, concat_axis=1, tiled=True)
    moved = moved.reshape(rows // count, count, 2, width // 2)
    return [moved[:, :, i].reshape(rows // count, count * width // 2) for i in range(2)]


def from_behind(value, axis, steps):
    count = lax.axis_size(axis)
    pairs = [(source, (source + steps) % count) for source in range(count)]
    return lax.ppermute(value, axis, pairs)


def attention_kernel(
    picks_ref, qd_ref, kv_ref, left_ref, right_ref,
    out_ref, own_grad_ref, to_left_ref, to_right_ref, left_acc, right_acc,
):
    number = pl.program_id(0)
    scale = HEAD_DIM ** (-0.5)
    f32 = jnp.float32

    @pl.when(number == 0)
    def _():
        left_acc[...] = jnp.zeros(left_acc.shape, f32)
        right_acc[...] = jnp.zeros(right_acc.shape, f32)

    packed = qd_ref[0]
    lane = lax.broadcasted_iota(jnp.int32, packed.shape, 1)
    low = lane < HEAD_DIM
    zero = jnp.zeros_like(packed)
    query_ext = jnp.where(low, packed, zero)
    grad_ext = jnp.where(low, zero, packed)
    pairs = (kv_ref[0], left_ref[0], right_ref[0])

    def nt(a, b):
        return lax.dot_general(a, b, (((1,), (1,)), ((), ())), preferred_element_type=f32)

    def nn(a, b):
        return lax.dot_general(a, b, (((1,), (0,)), ((), ())), preferred_element_type=f32)

    def tn(a, b):
        return lax.dot_general(a, b, (((0,), (0,)), ((), ())), preferred_element_type=f32)

    scores = [nt(query_ext, pair) * scale for pair in pairs]
    row = lax.broadcasted_iota(jnp.int32, scores[0].shape, 0)
    col = lax.broadcasted_iota(jnp.int32, scores[0].shape, 1)
    scores[0] = jnp.where(col <= row, scores[0], -jnp.inf)
    highest = jnp.max(scores[0], axis=1, keepdims=True)
    for part in scores[1:]:
        highest = jnp.maximum(highest, jnp.max(part, axis=1, keepdims=True))
    total = sum(jnp.sum(jnp.exp(part - highest), axis=1, keepdims=True) for part in scores)
    log_total = highest + jnp.log(total)
    weights = [jnp.exp(part - log_total) for part in scores]
    weights_bf = [w.astype(jnp.bfloat16) for w in weights]
    attended = sum(nn(w, pair) for w, pair in zip(weights_bf, pairs)).astype(jnp.bfloat16)
    products = jnp.where(low, 0.0, packed.astype(f32) * attended.astype(f32))
    row_delta = jnp.sum(products, axis=1, keepdims=True)
    score_grads = [
        (w * (nt(grad_ext, pair) - row_delta)).astype(jnp.bfloat16) for w, pair in zip(weights, pairs)
    ]
    query_grad = (sum(nn(d, pair) for d, pair in zip(score_grads, pairs)) * scale).astype(jnp.bfloat16)
    out_ref[0] = jnp.where(low, query_grad, attended)
    key_parts = [tn(d, packed) * scale for d in score_grads]
    value_parts = [tn(w, packed) for w in weights_bf]
    kv_parts = [jnp.where(low, k, v) for k, v in zip(key_parts, value_parts)]
    own_grad_ref[0] = kv_parts[0]
    left_pick = picks_ref[0, number]
    right_pick = picks_ref[1, number]
    left_acc[left_pick] += kv_parts[1]
    right_acc[right_pick] += kv_parts[2]

    @pl.when(number == pl.num_programs(0) - 1)
    def _():
        to_left_ref[...] = left_acc[...].astype(jnp.bfloat16)
        to_right_ref[...] = right_acc[...].astype(jnp.bfloat16)


def attention(picks, qd, kv, left, right):
    block_count, block, width = kv.shape
    left_spec = pl.BlockSpec((1, block, width), lambda n, p: (p[0, n], 0, 0))
    right_spec = pl.BlockSpec((1, block, width), lambda n, p: (p[1, n], 0, 0))
    one_spec = pl.BlockSpec((1, block, width), lambda n, p: (n, 0, 0))
    whole_spec = pl.BlockSpec((block_count, block, width), lambda n, p: (0, 0, 0))
    shape = (block_count, block, width)
    return pl.pallas_call(
        attention_kernel,
        grid_spec=pltpu.PrefetchScalarGridSpec(
            num_scalar_prefetch=1,
            grid=(block_count,),
            in_specs=[one_spec, one_spec, left_spec, right_spec],
            out_specs=[one_spec, one_spec, whole_spec, whole_spec],
            scratch_shapes=[pltpu.VMEM(shape, jnp.float32), pltpu.VMEM(shape, jnp.float32)],
        ),
        out_shape=[
            jax.ShapeDtypeStruct(shape, jnp.bfloat16),
            jax.ShapeDtypeStruct(shape, jnp.float32),
            jax.ShapeDtypeStruct(shape, jnp.bfloat16),
            jax.ShapeDtypeStruct(shape, jnp.bfloat16),
        ],
        compiler_params=pltpu.CompilerParams(dimension_semantics=("arbitrary",)),
        interpret=INTERPRET,
    )(picks, qd, kv, left, right)


def shards(query_rows, key_rows, value_rows, out_grad, neighbour_blocks):
    kv_heads = to_heads(key_rows, value_rows)
    row_count, width = kv_heads.shape
    block_count = row_count // BLOCK
    kv = kv_heads.reshape(block_count, BLOCK, width)
    left = from_behind(kv, "blk", 1)
    right = from_behind(kv, "blk", -1)
    qd = to_heads(query_rows, out_grad).reshape(block_count, BLOCK, width)
    first_row = lax.axis_index("blk") * block_count
    picks = jnp.stack(
        [lax.dynamic_slice_in_dim(neighbour_blocks[:, c], first_row, block_count, 0) for c in range(2)]
    )
    picks = jnp.clip(picks, 0, block_count - 1).astype(jnp.int32)
    out_pair, own_grads, to_left, to_right = attention(picks, qd, kv, left, right)
    from_right = from_behind(to_left, "blk", -1).astype(jnp.float32)
    from_left = from_behind(to_right, "blk", 1).astype(jnp.float32)
    query_grad, attended = to_rows(out_pair.reshape(row_count, width))
    kv_grads = (own_grads + from_right + from_left).astype(jnp.bfloat16)
    key_grad, value_grad = to_rows(kv_grads.reshape(row_count, width))
    return (attended, query_grad, key_grad, value_grad)


def solution(mesh):
    in_specs = (
        P(("blk", "head"), None),
        P(("blk", "head"), None),
        P(("blk", "head"), None),
        P(("blk", "head"), None),
        P(),
    )
    out_specs = (
        P(("blk", "head"), None),
        P(("blk", "head"), None),
        P(("blk", "head"), None),
        P(("blk", "head"), None),
    )
    return jax.shard_map(shards, mesh=mesh, in_specs=in_specs, out_specs=out_specs, check_vma=False)
```

```python
import jax
import jax.numpy as jnp
from jax import lax
from jax.experimental import pallas as pl
from jax.experimental.pallas import tpu as pltpu
from jax.sharding import PartitionSpec as P

HEAD_DIM = 64
BLOCK = 512
INTERPRET = False


def to_heads(first, second):
    count = lax.axis_size("head")
    rows, width = first.shape
    split = [a.reshape(rows, count, width // count) for a in (first, second)]
    packed = jnp.concatenate(split, axis=2)
    moved = lax.all_to_all(packed, "head", split_axis=1, concat_axis=0, tiled=True)
    return moved.reshape(count * rows, 2 * width // count)


def to_rows(packed):
    count = lax.axis_size("head")
    rows, width = packed.shape
    moved = lax.all_to_all(packed, "head", split_axis=0, concat_axis=1, tiled=True)
    moved = moved.reshape(rows // count, count, 2, width // 2)
    return [moved[:, :, i].reshape(rows // count, count * width // 2) for i in range(2)]


def from_behind(value, axis, steps):
    count = lax.axis_size(axis)
    pairs = [(source, (source + steps) % count) for source in range(count)]
    return lax.ppermute(value, axis, pairs)


def attention_kernel(
    picks_ref, qd_ref, kv_ref, left_ref, right_ref,
    out_ref, own_grad_ref, to_left_ref, to_right_ref, left_acc, right_acc,
):
    number = pl.program_id(0)
    scale = HEAD_DIM ** (-0.5)
    f32 = jnp.float32

    @pl.when(number == 0)
    def _():
        left_acc[...] = jnp.zeros(left_acc.shape, f32)
        right_acc[...] = jnp.zeros(right_acc.shape, f32)

    packed = qd_ref[0]
    lane = lax.broadcasted_iota(jnp.int32, packed.shape, 1)
    low = lane < HEAD_DIM
    zero = jnp.zeros_like(packed)
    query_ext = jnp.where(low, packed, zero)
    grad_ext = jnp.where(low, zero, packed)
    pairs = (kv_ref[0], left_ref[0], right_ref[0])

    def nt(a, b):
        return lax.dot_general(a, b, (((1,), (1,)), ((), ())), preferred_element_type=f32)

    def nn(a, b):
        return lax.dot_general(a, b, (((1,), (0,)), ((), ())), preferred_element_type=f32)

    def tn(a, b):
        return lax.dot_general(a, b, (((0,), (0,)), ((), ())), preferred_element_type=f32)

    scores = [nt(query_ext, pair) * scale for pair in pairs]
    row = lax.broadcasted_iota(jnp.int32, scores[0].shape, 0)
    col = lax.broadcasted_iota(jnp.int32, scores[0].shape, 1)
    scores[0] = jnp.where(col <= row, scores[0], -jnp.inf)
    highest = jnp.max(scores[0], axis=1, keepdims=True)
    for part in scores[1:]:
        highest = jnp.maximum(highest, jnp.max(part, axis=1, keepdims=True))
    shifted = [jnp.exp(part - highest) for part in scores]
    total = sum(jnp.sum(part, axis=1, keepdims=True) for part in shifted)
    inverse = 1.0 / total
    weights = [part * inverse for part in shifted]
    weights_bf = [w.astype(jnp.bfloat16) for w in weights]
    attended = sum(nn(w, pair) for w, pair in zip(weights_bf, pairs)).astype(jnp.bfloat16)
    products = jnp.where(low, 0.0, packed.astype(f32) * attended.astype(f32))
    row_delta = jnp.sum(products, axis=1, keepdims=True)
    score_grads = [
        (w * (nt(grad_ext, pair) - row_delta)).astype(jnp.bfloat16) for w, pair in zip(weights, pairs)
    ]
    query_grad = (sum(nn(d, pair) for d, pair in zip(score_grads, pairs)) * scale).astype(jnp.bfloat16)
    out_ref[0] = jnp.where(low, query_grad, attended)
    key_parts = [tn(d, packed) * scale for d in score_grads]
    value_parts = [tn(w, packed) for w in weights_bf]
    kv_parts = [jnp.where(low, k, v) for k, v in zip(key_parts, value_parts)]
    own_grad_ref[0] = kv_parts[0]
    left_pick = picks_ref[0, number]
    right_pick = picks_ref[1, number]
    left_acc[left_pick] += kv_parts[1]
    right_acc[right_pick] += kv_parts[2]

    @pl.when(number == pl.num_programs(0) - 1)
    def _():
        to_left_ref[...] = left_acc[...].astype(jnp.bfloat16)
        to_right_ref[...] = right_acc[...].astype(jnp.bfloat16)


def attention(picks, qd, kv, left, right):
    block_count, block, width = kv.shape
    left_spec = pl.BlockSpec((1, block, width), lambda n, p: (p[0, n], 0, 0))
    right_spec = pl.BlockSpec((1, block, width), lambda n, p: (p[1, n], 0, 0))
    one_spec = pl.BlockSpec((1, block, width), lambda n, p: (n, 0, 0))
    whole_spec = pl.BlockSpec((block_count, block, width), lambda n, p: (0, 0, 0))
    shape = (block_count, block, width)
    return pl.pallas_call(
        attention_kernel,
        grid_spec=pltpu.PrefetchScalarGridSpec(
            num_scalar_prefetch=1,
            grid=(block_count,),
            in_specs=[one_spec, one_spec, left_spec, right_spec],
            out_specs=[one_spec, one_spec, whole_spec, whole_spec],
            scratch_shapes=[pltpu.VMEM(shape, jnp.float32), pltpu.VMEM(shape, jnp.float32)],
        ),
        out_shape=[
            jax.ShapeDtypeStruct(shape, jnp.bfloat16),
            jax.ShapeDtypeStruct(shape, jnp.float32),
            jax.ShapeDtypeStruct(shape, jnp.bfloat16),
            jax.ShapeDtypeStruct(shape, jnp.bfloat16),
        ],
        compiler_params=pltpu.CompilerParams(dimension_semantics=("arbitrary",)),
        interpret=INTERPRET,
    )(picks, qd, kv, left, right)


def shards(query_rows, key_rows, value_rows, out_grad, neighbour_blocks):
    kv_heads = to_heads(key_rows, value_rows)
    row_count, width = kv_heads.shape
    block_count = row_count // BLOCK
    kv = kv_heads.reshape(block_count, BLOCK, width)
    left = from_behind(kv, "blk", 1)
    right = from_behind(kv, "blk", -1)
    qd = to_heads(query_rows, out_grad).reshape(block_count, BLOCK, width)
    first_row = lax.axis_index("blk") * block_count
    picks = jnp.stack(
        [lax.dynamic_slice_in_dim(neighbour_blocks[:, c], first_row, block_count, 0) for c in range(2)]
    )
    picks = jnp.clip(picks, 0, block_count - 1).astype(jnp.int32)
    out_pair, own_grads, to_left, to_right = attention(picks, qd, kv, left, right)
    from_right = from_behind(to_left, "blk", -1).astype(jnp.float32)
    from_left = from_behind(to_right, "blk", 1).astype(jnp.float32)
    query_grad, attended = to_rows(out_pair.reshape(row_count, width))
    kv_grads = (own_grads + from_right + from_left).astype(jnp.bfloat16)
    key_grad, value_grad = to_rows(kv_grads.reshape(row_count, width))
    return (attended, query_grad, key_grad, value_grad)


def solution(mesh):
    in_specs = (
        P(("blk", "head"), None),
        P(("blk", "head"), None),
        P(("blk", "head"), None),
        P(("blk", "head"), None),
        P(),
    )
    out_specs = (
        P(("blk", "head"), None),
        P(("blk", "head"), None),
        P(("blk", "head"), None),
        P(("blk", "head"), None),
    )
    return jax.shard_map(shards, mesh=mesh, in_specs=in_specs, out_specs=out_specs, check_vma=False)
```

```python
import jax
import jax.numpy as jnp
from jax import lax
from jax.experimental import pallas as pl
from jax.experimental.pallas import tpu as pltpu
from jax.sharding import PartitionSpec as P

HEAD_DIM = 64
BLOCK = 512
INTERPRET = False


def to_heads(first, second):
    count = lax.axis_size("head")
    rows, width = first.shape
    split = [a.reshape(rows, count, width // count) for a in (first, second)]
    packed = jnp.concatenate(split, axis=2)
    moved = lax.all_to_all(packed, "head", split_axis=1, concat_axis=0, tiled=True)
    return moved.reshape(count * rows, 2 * width // count)


def to_rows(packed):
    count = lax.axis_size("head")
    rows, width = packed.shape
    moved = lax.all_to_all(packed, "head", split_axis=0, concat_axis=1, tiled=True)
    moved = moved.reshape(rows // count, count, 2, width // 2)
    return [moved[:, :, i].reshape(rows // count, count * width // 2) for i in range(2)]


def from_behind(value, axis, steps):
    count = lax.axis_size(axis)
    pairs = [(source, (source + steps) % count) for source in range(count)]
    return lax.ppermute(value, axis, pairs)


def attention_kernel(
    picks_ref, qd_ref, kv_ref, left_ref, right_ref,
    out_ref, highest_ref, inverse_ref, delta_ref, to_left_ref, to_right_ref, left_acc, right_acc,
):
    number = pl.program_id(0)
    scale = HEAD_DIM ** (-0.5)
    f32 = jnp.float32

    @pl.when(number == 0)
    def _():
        left_acc[...] = jnp.zeros(left_acc.shape, f32)
        right_acc[...] = jnp.zeros(right_acc.shape, f32)

    packed = qd_ref[0]
    lane = lax.broadcasted_iota(jnp.int32, packed.shape, 1)
    low = lane < HEAD_DIM
    zero = jnp.zeros_like(packed)
    query_ext = jnp.where(low, packed, zero)
    grad_ext = jnp.where(low, zero, packed)
    pairs = (kv_ref[0], left_ref[0], right_ref[0])

    def nt(a, b):
        return lax.dot_general(a, b, (((1,), (1,)), ((), ())), preferred_element_type=f32)

    def nn(a, b):
        return lax.dot_general(a, b, (((1,), (0,)), ((), ())), preferred_element_type=f32)

    def tn(a, b):
        return lax.dot_general(a, b, (((0,), (0,)), ((), ())), preferred_element_type=f32)

    scores = [nt(query_ext, pair) * scale for pair in pairs]
    row = lax.broadcasted_iota(jnp.int32, scores[0].shape, 0)
    col = lax.broadcasted_iota(jnp.int32, scores[0].shape, 1)
    scores[0] = jnp.where(col <= row, scores[0], -jnp.inf)
    highest = jnp.max(scores[0], axis=1, keepdims=True)
    for part in scores[1:]:
        highest = jnp.maximum(highest, jnp.max(part, axis=1, keepdims=True))
    shifted = [jnp.exp(part - highest) for part in scores]
    total = sum(jnp.sum(part, axis=1, keepdims=True) for part in shifted)
    inverse = 1.0 / total
    weights = [part * inverse for part in shifted]
    weights_bf = [w.astype(jnp.bfloat16) for w in weights]
    attended = sum(nn(w, pair) for w, pair in zip(weights_bf, pairs)).astype(jnp.bfloat16)
    products = jnp.where(low, 0.0, packed.astype(f32) * attended.astype(f32))
    row_delta = jnp.sum(products, axis=1, keepdims=True)
    score_grads = [
        (w * (nt(grad_ext, pair) - row_delta)).astype(jnp.bfloat16) for w, pair in zip(weights, pairs)
    ]
    query_grad = (sum(nn(d, pair) for d, pair in zip(score_grads, pairs)) * scale).astype(jnp.bfloat16)
    out_ref[0] = jnp.where(low, query_grad, attended)
    highest_ref[0] = highest
    inverse_ref[0] = inverse
    delta_ref[0] = row_delta
    kv_parts = [None] + [
        jnp.where(low, tn(d, packed) * scale, tn(w, packed))
        for d, w in zip(score_grads[1:], weights_bf[1:])
    ]
    left_pick = picks_ref[0, number]
    right_pick = picks_ref[1, number]
    left_acc[left_pick] += kv_parts[1]
    right_acc[right_pick] += kv_parts[2]

    @pl.when(number == pl.num_programs(0) - 1)
    def _():
        to_left_ref[...] = left_acc[...].astype(jnp.bfloat16)
        to_right_ref[...] = right_acc[...].astype(jnp.bfloat16)


def own_kernel(qd_ref, kv_ref, highest_ref, inverse_ref, delta_ref, own_grad_ref):
    scale = HEAD_DIM ** (-0.5)
    f32 = jnp.float32
    packed = qd_ref[0]
    pair = kv_ref[0]
    lane = lax.broadcasted_iota(jnp.int32, packed.shape, 1)
    low = lane < HEAD_DIM
    zero = jnp.zeros_like(packed)
    query_ext = jnp.where(low, packed, zero)
    grad_ext = jnp.where(low, zero, packed)
    score = lax.dot_general(query_ext, pair, (((1,), (1,)), ((), ())), preferred_element_type=f32) * scale
    row = lax.broadcasted_iota(jnp.int32, score.shape, 0)
    col = lax.broadcasted_iota(jnp.int32, score.shape, 1)
    score = jnp.where(col <= row, score, -jnp.inf)
    weight = jnp.exp(score - highest_ref[0]) * inverse_ref[0]
    weight_grad = lax.dot_general(grad_ext, pair, (((1,), (1,)), ((), ())), preferred_element_type=f32)
    score_grad = (weight * (weight_grad - delta_ref[0])).astype(jnp.bfloat16)
    key_part = lax.dot_general(score_grad, packed, (((0,), (0,)), ((), ())), preferred_element_type=f32)
    value_part = lax.dot_general(
        weight.astype(jnp.bfloat16), packed, (((0,), (0,)), ((), ())), preferred_element_type=f32
    )
    own_grad_ref[0] = jnp.where(low, key_part * scale, value_part)


def own_grads_of(qd, kv, highest, inverse, delta):
    block_count, block, width = kv.shape
    one_spec = pl.BlockSpec((1, block, width), lambda n: (n, 0, 0))
    stat_spec = pl.BlockSpec((1, block, 1), lambda n: (n, 0, 0))
    return pl.pallas_call(
        own_kernel,
        grid=(block_count,),
        in_specs=[one_spec, one_spec, stat_spec, stat_spec, stat_spec],
        out_specs=one_spec,
        out_shape=jax.ShapeDtypeStruct((block_count, block, width), jnp.float32),
        compiler_params=pltpu.CompilerParams(dimension_semantics=("arbitrary",)),
        interpret=INTERPRET,
    )(qd, kv, highest, inverse, delta)


def attention(picks, qd, kv, left, right):
    block_count, block, width = kv.shape
    left_spec = pl.BlockSpec((1, block, width), lambda n, p: (p[0, n], 0, 0))
    right_spec = pl.BlockSpec((1, block, width), lambda n, p: (p[1, n], 0, 0))
    one_spec = pl.BlockSpec((1, block, width), lambda n, p: (n, 0, 0))
    whole_spec = pl.BlockSpec((block_count, block, width), lambda n, p: (0, 0, 0))
    stat_spec = pl.BlockSpec((1, block, 1), lambda n, p: (n, 0, 0))
    shape = (block_count, block, width)
    stat = jax.ShapeDtypeStruct((block_count, block, 1), jnp.float32)
    return pl.pallas_call(
        attention_kernel,
        grid_spec=pltpu.PrefetchScalarGridSpec(
            num_scalar_prefetch=1,
            grid=(block_count,),
            in_specs=[one_spec, one_spec, left_spec, right_spec],
            out_specs=[one_spec, stat_spec, stat_spec, stat_spec, whole_spec, whole_spec],
            scratch_shapes=[pltpu.VMEM(shape, jnp.float32), pltpu.VMEM(shape, jnp.float32)],
        ),
        out_shape=[
            jax.ShapeDtypeStruct(shape, jnp.bfloat16),
            stat,
            stat,
            stat,
            jax.ShapeDtypeStruct(shape, jnp.bfloat16),
            jax.ShapeDtypeStruct(shape, jnp.bfloat16),
        ],
        compiler_params=pltpu.CompilerParams(dimension_semantics=("arbitrary",)),
        interpret=INTERPRET,
    )(picks, qd, kv, left, right)


def shards(query_rows, key_rows, value_rows, out_grad, neighbour_blocks):
    kv_heads = to_heads(key_rows, value_rows)
    row_count, width = kv_heads.shape
    block_count = row_count // BLOCK
    kv = kv_heads.reshape(block_count, BLOCK, width)
    left = from_behind(kv, "blk", 1)
    right = from_behind(kv, "blk", -1)
    qd = to_heads(query_rows, out_grad).reshape(block_count, BLOCK, width)
    first_row = lax.axis_index("blk") * block_count
    picks = jnp.stack(
        [lax.dynamic_slice_in_dim(neighbour_blocks[:, c], first_row, block_count, 0) for c in range(2)]
    )
    picks = jnp.clip(picks, 0, block_count - 1).astype(jnp.int32)
    out_pair, highest, inverse, delta, to_left, to_right = attention(picks, qd, kv, left, right)
    from_right = from_behind(to_left, "blk", -1).astype(jnp.float32)
    from_left = from_behind(to_right, "blk", 1).astype(jnp.float32)
    own_grads = own_grads_of(qd, kv, highest, inverse, delta)
    query_grad, attended = to_rows(out_pair.reshape(row_count, width))
    kv_grads = (own_grads + from_right + from_left).astype(jnp.bfloat16)
    key_grad, value_grad = to_rows(kv_grads.reshape(row_count, width))
    return (attended, query_grad, key_grad, value_grad)


def solution(mesh):
    in_specs = (
        P(("blk", "head"), None),
        P(("blk", "head"), None),
        P(("blk", "head"), None),
        P(("blk", "head"), None),
        P(),
    )
    out_specs = (
        P(("blk", "head"), None),
        P(("blk", "head"), None),
        P(("blk", "head"), None),
        P(("blk", "head"), None),
    )
    return jax.shard_map(shards, mesh=mesh, in_specs=in_specs, out_specs=out_specs, check_vma=False)
```

```python
import jax
import jax.numpy as jnp
from jax import lax
from jax.experimental import pallas as pl
from jax.experimental.pallas import tpu as pltpu
from jax.sharding import PartitionSpec as P

HEAD_DIM = 64
BLOCK = 512
INTERPRET = False


def to_heads(first, second):
    count = lax.axis_size("head")
    rows, width = first.shape
    split = [a.reshape(rows, count, width // count) for a in (first, second)]
    packed = jnp.concatenate(split, axis=2)
    moved = lax.all_to_all(packed, "head", split_axis=1, concat_axis=0, tiled=True)
    return moved.reshape(count * rows, 2 * width // count)


def to_rows(packed):
    count = lax.axis_size("head")
    rows, width = packed.shape
    moved = lax.all_to_all(packed, "head", split_axis=0, concat_axis=1, tiled=True)
    moved = moved.reshape(rows // count, count, 2, width // 2)
    return [moved[:, :, i].reshape(rows // count, count * width // 2) for i in range(2)]


def from_behind(value, axis, steps):
    count = lax.axis_size(axis)
    pairs = [(source, (source + steps) % count) for source in range(count)]
    return lax.ppermute(value, axis, pairs)


def attention_kernel(
    picks_ref, qd_ref, kv_ref, left_ref, right_ref,
    out_ref, highest_ref, inverse_ref, delta_ref, to_left_ref, to_right_ref, left_acc, right_acc,
):
    number = pl.program_id(0)
    scale = HEAD_DIM ** (-0.5)
    f32 = jnp.float32

    @pl.when(number == 0)
    def _():
        left_acc[...] = jnp.zeros(left_acc.shape, f32)
        right_acc[...] = jnp.zeros(right_acc.shape, f32)

    packed = qd_ref[0]
    lane = lax.broadcasted_iota(jnp.int32, packed.shape, 1)
    low = lane < HEAD_DIM
    zero = jnp.zeros_like(packed)
    query_ext = jnp.where(low, packed, zero)
    grad_ext = jnp.where(low, zero, packed)
    pairs = (kv_ref[0], left_ref[0], right_ref[0])

    def nt(a, b):
        return lax.dot_general(a, b, (((1,), (1,)), ((), ())), preferred_element_type=f32)

    def nn(a, b):
        return lax.dot_general(a, b, (((1,), (0,)), ((), ())), preferred_element_type=f32)

    def tn(a, b):
        return lax.dot_general(a, b, (((0,), (0,)), ((), ())), preferred_element_type=f32)

    scores = [nt(query_ext, pair) * scale for pair in pairs]
    row = lax.broadcasted_iota(jnp.int32, scores[0].shape, 0)
    col = lax.broadcasted_iota(jnp.int32, scores[0].shape, 1)
    scores[0] = jnp.where(col <= row, scores[0], -jnp.inf)
    highest = jnp.max(scores[0], axis=1, keepdims=True)
    for part in scores[1:]:
        highest = jnp.maximum(highest, jnp.max(part, axis=1, keepdims=True))
    shifted = [jnp.exp(part - highest) for part in scores]
    total = sum(jnp.sum(part, axis=1, keepdims=True) for part in shifted)
    inverse = 1.0 / total
    weights = [part * inverse for part in shifted]
    weights_bf = [w.astype(jnp.bfloat16) for w in weights]
    attended = sum(nn(w, pair) for w, pair in zip(weights_bf, pairs)).astype(jnp.bfloat16)
    products = jnp.where(low, 0.0, packed.astype(f32) * attended.astype(f32))
    row_delta = jnp.sum(products, axis=1, keepdims=True)
    score_grads = [
        (w * (nt(grad_ext, pair) - row_delta)).astype(jnp.bfloat16) for w, pair in zip(weights, pairs)
    ]
    query_grad = (sum(nn(d, pair) for d, pair in zip(score_grads, pairs)) * scale).astype(jnp.bfloat16)
    out_ref[0] = jnp.where(low, query_grad, attended)
    highest_ref[0] = highest
    inverse_ref[0] = inverse
    delta_ref[0] = row_delta
    kv_parts = [None] + [
        jnp.where(low, tn(d, packed) * scale, tn(w, packed))
        for d, w in zip(score_grads[1:], weights_bf[1:])
    ]
    left_pick = picks_ref[0, number]
    right_pick = picks_ref[1, number]
    left_acc[left_pick] += kv_parts[1]
    right_acc[right_pick] += kv_parts[2]

    @pl.when(number == pl.num_programs(0) - 1)
    def _():
        to_left_ref[...] = left_acc[...].astype(jnp.bfloat16)
        to_right_ref[...] = right_acc[...].astype(jnp.bfloat16)


def own_kernel(qd_ref, kv_ref, highest_ref, inverse_ref, delta_ref, own_grad_ref):
    scale = HEAD_DIM ** (-0.5)
    f32 = jnp.float32
    packed = qd_ref[0]
    pair = kv_ref[0]
    lane = lax.broadcasted_iota(jnp.int32, packed.shape, 1)
    low = lane < HEAD_DIM
    zero = jnp.zeros_like(packed)
    query_ext = jnp.where(low, packed, zero)
    grad_ext = jnp.where(low, zero, packed)
    score = lax.dot_general(query_ext, pair, (((1,), (1,)), ((), ())), preferred_element_type=f32) * scale
    row = lax.broadcasted_iota(jnp.int32, score.shape, 0)
    col = lax.broadcasted_iota(jnp.int32, score.shape, 1)
    score = jnp.where(col <= row, score, -jnp.inf)
    weight = jnp.exp(score - highest_ref[0]) * inverse_ref[0]
    weight_grad = lax.dot_general(grad_ext, pair, (((1,), (1,)), ((), ())), preferred_element_type=f32)
    score_grad = (weight * (weight_grad - delta_ref[0])).astype(jnp.bfloat16)
    key_part = lax.dot_general(score_grad, packed, (((0,), (0,)), ((), ())), preferred_element_type=f32)
    value_part = lax.dot_general(
        weight.astype(jnp.bfloat16), packed, (((0,), (0,)), ((), ())), preferred_element_type=f32
    )
    own_grad_ref[0] = jnp.where(low, key_part * scale, value_part)


def own_grads_of(qd, kv, highest, inverse, delta):
    block_count, block, width = kv.shape
    one_spec = pl.BlockSpec((1, block, width), lambda n: (n, 0, 0))
    stat_spec = pl.BlockSpec((1, block, 1), lambda n: (n, 0, 0))
    return pl.pallas_call(
        own_kernel,
        grid=(block_count,),
        in_specs=[one_spec, one_spec, stat_spec, stat_spec, stat_spec],
        out_specs=one_spec,
        out_shape=jax.ShapeDtypeStruct((block_count, block, width), jnp.float32),
        compiler_params=pltpu.CompilerParams(dimension_semantics=("arbitrary",)),
        interpret=INTERPRET,
    )(qd, kv, highest, inverse, delta)


def attention(picks, qd, kv, left, right):
    block_count, block, width = kv.shape
    left_spec = pl.BlockSpec((1, block, width), lambda n, p: (p[0, n], 0, 0))
    right_spec = pl.BlockSpec((1, block, width), lambda n, p: (p[1, n], 0, 0))
    one_spec = pl.BlockSpec((1, block, width), lambda n, p: (n, 0, 0))
    whole_spec = pl.BlockSpec((block_count, block, width), lambda n, p: (0, 0, 0))
    stat_spec = pl.BlockSpec((1, block, 1), lambda n, p: (n, 0, 0))
    shape = (block_count, block, width)
    stat = jax.ShapeDtypeStruct((block_count, block, 1), jnp.float32)
    return pl.pallas_call(
        attention_kernel,
        grid_spec=pltpu.PrefetchScalarGridSpec(
            num_scalar_prefetch=1,
            grid=(block_count,),
            in_specs=[one_spec, one_spec, left_spec, right_spec],
            out_specs=[one_spec, stat_spec, stat_spec, stat_spec, whole_spec, whole_spec],
            scratch_shapes=[pltpu.VMEM(shape, jnp.float32), pltpu.VMEM(shape, jnp.float32)],
        ),
        out_shape=[
            jax.ShapeDtypeStruct(shape, jnp.bfloat16),
            stat,
            stat,
            stat,
            jax.ShapeDtypeStruct(shape, jnp.bfloat16),
            jax.ShapeDtypeStruct(shape, jnp.bfloat16),
        ],
        compiler_params=pltpu.CompilerParams(dimension_semantics=("arbitrary",)),
        interpret=INTERPRET,
    )(picks, qd, kv, left, right)


def shards(query_rows, key_rows, value_rows, out_grad, neighbour_blocks):
    kv_heads = to_heads(key_rows, value_rows)
    row_count, width = kv_heads.shape
    block_count = row_count // BLOCK
    kv = kv_heads.reshape(block_count, BLOCK, width)
    count = lax.axis_size("blk")
    near_pairs = [(i, i ^ 1) for i in range(count)]
    far_pairs = [(i, (i + 1 if i % 2 else i - 1) % count) for i in range(count)]
    near = lax.ppermute(kv, "blk", near_pairs)
    far = lax.ppermute(kv, "blk", far_pairs)
    qd = to_heads(query_rows, out_grad).reshape(block_count, BLOCK, width)
    place = lax.axis_index("blk")
    first_row = place * block_count
    picks = [lax.dynamic_slice_in_dim(neighbour_blocks[:, c], first_row, block_count, 0) for c in range(2)]
    even = place % 2 == 0
    picks = jnp.stack([jnp.where(even, picks[1], picks[0]), jnp.where(even, picks[0], picks[1])])
    picks = jnp.clip(picks, 0, block_count - 1).astype(jnp.int32)
    out_pair, highest, inverse, delta, to_near, to_far = attention(picks, qd, kv, near, far)
    from_near = lax.ppermute(to_near, "blk", near_pairs).astype(jnp.float32)
    from_far = lax.ppermute(to_far, "blk", far_pairs).astype(jnp.float32)
    own_grads = own_grads_of(qd, kv, highest, inverse, delta)
    query_grad, attended = to_rows(out_pair.reshape(row_count, width))
    kv_grads = (own_grads + from_near + from_far).astype(jnp.bfloat16)
    key_grad, value_grad = to_rows(kv_grads.reshape(row_count, width))
    return (attended, query_grad, key_grad, value_grad)


def solution(mesh):
    in_specs = (
        P(("blk", "head"), None),
        P(("blk", "head"), None),
        P(("blk", "head"), None),
        P(("blk", "head"), None),
        P(),
    )
    out_specs = (
        P(("blk", "head"), None),
        P(("blk", "head"), None),
        P(("blk", "head"), None),
        P(("blk", "head"), None),
    )
    return jax.shard_map(shards, mesh=mesh, in_specs=in_specs, out_specs=out_specs, check_vma=False)
```

```python
import jax
import jax.numpy as jnp
from jax import lax
from jax.experimental import pallas as pl
from jax.experimental.pallas import tpu as pltpu
from jax.sharding import PartitionSpec as P

HEAD_DIM = 64
BLOCK = 512
INTERPRET = False


def to_heads(first, second):
    count = lax.axis_size("head")
    rows, width = first.shape
    split = [a.reshape(rows, count, width // count) for a in (first, second)]
    packed = jnp.concatenate(split, axis=2)
    moved = lax.all_to_all(packed, "head", split_axis=1, concat_axis=0, tiled=True)
    return moved.reshape(count * rows, 2 * width // count)


def to_rows(packed):
    count = lax.axis_size("head")
    rows, width = packed.shape
    moved = lax.all_to_all(packed, "head", split_axis=0, concat_axis=1, tiled=True)
    moved = moved.reshape(rows // count, count, 2, width // 2)
    return [moved[:, :, i].reshape(rows // count, count * width // 2) for i in range(2)]


def from_behind(value, axis, steps):
    count = lax.axis_size(axis)
    pairs = [(source, (source + steps) % count) for source in range(count)]
    return lax.ppermute(value, axis, pairs)


def attention_kernel(
    picks_ref, qd_ref, kv_ref, left_ref, right_ref,
    out_ref, highest_ref, inverse_ref, delta_ref, to_left_ref, to_right_ref, left_acc, right_acc,
):
    number = pl.program_id(0)
    half = pl.program_id(1)
    scale = HEAD_DIM ** (-0.5)
    f32 = jnp.float32

    @pl.when((number == 0) & (half == 0))
    def _():
        left_acc[...] = jnp.zeros(left_acc.shape, f32)
        right_acc[...] = jnp.zeros(right_acc.shape, f32)

    packed = qd_ref[0]
    lane = lax.broadcasted_iota(jnp.int32, packed.shape, 1)
    low = lane < HEAD_DIM
    zero = jnp.zeros_like(packed)
    query_ext = jnp.where(low, packed, zero)
    grad_ext = jnp.where(low, zero, packed)
    pairs = (kv_ref[0], left_ref[0], right_ref[0])

    def nt(a, b):
        return lax.dot_general(a, b, (((1,), (1,)), ((), ())), preferred_element_type=f32)

    def nn(a, b):
        return lax.dot_general(a, b, (((1,), (0,)), ((), ())), preferred_element_type=f32)

    def tn(a, b):
        return lax.dot_general(a, b, (((0,), (0,)), ((), ())), preferred_element_type=f32)

    scores = [nt(query_ext, pair) * scale for pair in pairs]
    row = lax.broadcasted_iota(jnp.int32, scores[0].shape, 0) + half * packed.shape[0]
    col = lax.broadcasted_iota(jnp.int32, scores[0].shape, 1)
    scores[0] = jnp.where(col <= row, scores[0], -jnp.inf)
    highest = jnp.max(scores[0], axis=1, keepdims=True)
    for part in scores[1:]:
        highest = jnp.maximum(highest, jnp.max(part, axis=1, keepdims=True))
    shifted = [jnp.exp(part - highest) for part in scores]
    total = sum(jnp.sum(part, axis=1, keepdims=True) for part in shifted)
    inverse = 1.0 / total
    weights = [part * inverse for part in shifted]
    weights_bf = [w.astype(jnp.bfloat16) for w in weights]
    attended = sum(nn(w, pair) for w, pair in zip(weights_bf, pairs)).astype(jnp.bfloat16)
    products = jnp.where(low, 0.0, packed.astype(f32) * attended.astype(f32))
    row_delta = jnp.sum(products, axis=1, keepdims=True)
    score_grads = [
        (w * (nt(grad_ext, pair) - row_delta)).astype(jnp.bfloat16) for w, pair in zip(weights, pairs)
    ]
    query_grad = (sum(nn(d, pair) for d, pair in zip(score_grads, pairs)) * scale).astype(jnp.bfloat16)
    out_ref[0] = jnp.where(low, query_grad, attended)
    highest_ref[0] = highest
    inverse_ref[0] = inverse
    delta_ref[0] = row_delta
    key_low = lax.broadcasted_iota(jnp.int32, pairs[0].shape, 1) < HEAD_DIM
    kv_parts = [None] + [
        jnp.where(key_low, tn(d, packed) * scale, tn(w, packed))
        for d, w in zip(score_grads[1:], weights_bf[1:])
    ]
    left_pick = picks_ref[0, number]
    right_pick = picks_ref[1, number]
    left_acc[left_pick] += kv_parts[1]
    right_acc[right_pick] += kv_parts[2]

    @pl.when((number == pl.num_programs(0) - 1) & (half == pl.num_programs(1) - 1))
    def _():
        to_left_ref[...] = left_acc[...].astype(jnp.bfloat16)
        to_right_ref[...] = right_acc[...].astype(jnp.bfloat16)


def own_kernel(qd_ref, kv_ref, highest_ref, inverse_ref, delta_ref, own_grad_ref):
    scale = HEAD_DIM ** (-0.5)
    f32 = jnp.float32
    packed = qd_ref[0]
    pair = kv_ref[0]
    lane = lax.broadcasted_iota(jnp.int32, packed.shape, 1)
    low = lane < HEAD_DIM
    zero = jnp.zeros_like(packed)
    query_ext = jnp.where(low, packed, zero)
    grad_ext = jnp.where(low, zero, packed)
    score = lax.dot_general(query_ext, pair, (((1,), (1,)), ((), ())), preferred_element_type=f32) * scale
    row = lax.broadcasted_iota(jnp.int32, score.shape, 0)
    col = lax.broadcasted_iota(jnp.int32, score.shape, 1)
    score = jnp.where(col <= row, score, -jnp.inf)
    weight = jnp.exp(score - highest_ref[0]) * inverse_ref[0]
    weight_grad = lax.dot_general(grad_ext, pair, (((1,), (1,)), ((), ())), preferred_element_type=f32)
    score_grad = (weight * (weight_grad - delta_ref[0])).astype(jnp.bfloat16)
    key_part = lax.dot_general(score_grad, packed, (((0,), (0,)), ((), ())), preferred_element_type=f32)
    value_part = lax.dot_general(
        weight.astype(jnp.bfloat16), packed, (((0,), (0,)), ((), ())), preferred_element_type=f32
    )
    own_grad_ref[0] = jnp.where(low, key_part * scale, value_part)


def own_grads_of(qd, kv, highest, inverse, delta):
    block_count, block, width = kv.shape
    one_spec = pl.BlockSpec((1, block, width), lambda n: (n, 0, 0))
    stat_spec = pl.BlockSpec((1, block, 1), lambda n: (n, 0, 0))
    return pl.pallas_call(
        own_kernel,
        grid=(block_count,),
        in_specs=[one_spec, one_spec, stat_spec, stat_spec, stat_spec],
        out_specs=one_spec,
        out_shape=jax.ShapeDtypeStruct((block_count, block, width), jnp.float32),
        compiler_params=pltpu.CompilerParams(dimension_semantics=("arbitrary",)),
        interpret=INTERPRET,
    )(qd, kv, highest, inverse, delta)


def attention(picks, qd, kv, left, right):
    block_count, block, width = kv.shape
    tile = block // 2
    left_spec = pl.BlockSpec((1, block, width), lambda n, h, p: (p[0, n], 0, 0))
    right_spec = pl.BlockSpec((1, block, width), lambda n, h, p: (p[1, n], 0, 0))
    kv_spec = pl.BlockSpec((1, block, width), lambda n, h, p: (n, 0, 0))
    tile_spec = pl.BlockSpec((1, tile, width), lambda n, h, p: (n, h, 0))
    whole_spec = pl.BlockSpec((block_count, block, width), lambda n, h, p: (0, 0, 0))
    stat_spec = pl.BlockSpec((1, tile, 1), lambda n, h, p: (n, h, 0))
    shape = (block_count, block, width)
    stat = jax.ShapeDtypeStruct((block_count, block, 1), jnp.float32)
    return pl.pallas_call(
        attention_kernel,
        grid_spec=pltpu.PrefetchScalarGridSpec(
            num_scalar_prefetch=1,
            grid=(block_count, 2),
            in_specs=[tile_spec, kv_spec, left_spec, right_spec],
            out_specs=[tile_spec, stat_spec, stat_spec, stat_spec, whole_spec, whole_spec],
            scratch_shapes=[pltpu.VMEM(shape, jnp.float32), pltpu.VMEM(shape, jnp.float32)],
        ),
        out_shape=[
            jax.ShapeDtypeStruct(shape, jnp.bfloat16),
            stat,
            stat,
            stat,
            jax.ShapeDtypeStruct(shape, jnp.bfloat16),
            jax.ShapeDtypeStruct(shape, jnp.bfloat16),
        ],
        compiler_params=pltpu.CompilerParams(dimension_semantics=("arbitrary", "arbitrary")),
        interpret=INTERPRET,
    )(picks, qd, kv, left, right)


def shards(query_rows, key_rows, value_rows, out_grad, neighbour_blocks):
    kv_heads = to_heads(key_rows, value_rows)
    row_count, width = kv_heads.shape
    block_count = row_count // BLOCK
    kv = kv_heads.reshape(block_count, BLOCK, width)
    count = lax.axis_size("blk")
    near_pairs = [(i, i ^ 1) for i in range(count)]
    far_pairs = [(i, (i + 1 if i % 2 else i - 1) % count) for i in range(count)]
    near = lax.ppermute(kv, "blk", near_pairs)
    far = lax.ppermute(kv, "blk", far_pairs)
    qd = to_heads(query_rows, out_grad).reshape(block_count, BLOCK, width)
    place = lax.axis_index("blk")
    first_row = place * block_count
    picks = [lax.dynamic_slice_in_dim(neighbour_blocks[:, c], first_row, block_count, 0) for c in range(2)]
    even = place % 2 == 0
    picks = jnp.stack([jnp.where(even, picks[1], picks[0]), jnp.where(even, picks[0], picks[1])])
    picks = jnp.clip(picks, 0, block_count - 1).astype(jnp.int32)
    out_pair, highest, inverse, delta, to_near, to_far = attention(picks, qd, kv, near, far)
    from_near = lax.ppermute(to_near, "blk", near_pairs).astype(jnp.float32)
    from_far = lax.ppermute(to_far, "blk", far_pairs).astype(jnp.float32)
    own_grads = own_grads_of(qd, kv, highest, inverse, delta)
    query_grad, attended = to_rows(out_pair.reshape(row_count, width))
    kv_grads = (own_grads + from_near + from_far).astype(jnp.bfloat16)
    key_grad, value_grad = to_rows(kv_grads.reshape(row_count, width))
    return (attended, query_grad, key_grad, value_grad)


def solution(mesh):
    in_specs = (
        P(("blk", "head"), None),
        P(("blk", "head"), None),
        P(("blk", "head"), None),
        P(("blk", "head"), None),
        P(),
    )
    out_specs = (
        P(("blk", "head"), None),
        P(("blk", "head"), None),
        P(("blk", "head"), None),
        P(("blk", "head"), None),
    )
    return jax.shard_map(shards, mesh=mesh, in_specs=in_specs, out_specs=out_specs, check_vma=False)
```

```python
import jax
import jax.numpy as jnp
from jax import lax
from jax.experimental import pallas as pl
from jax.experimental.pallas import tpu as pltpu
from jax.sharding import PartitionSpec as P

HEAD_DIM = 64
BLOCK = 512
INTERPRET = False


def to_heads(first, second):
    count = lax.axis_size("head")
    rows, width = first.shape
    split = [a.reshape(rows, count, width // count) for a in (first, second)]
    packed = jnp.concatenate(split, axis=2)
    moved = lax.all_to_all(packed, "head", split_axis=1, concat_axis=0, tiled=True)
    return moved.reshape(count * rows, 2 * width // count)


def to_rows(packed):
    count = lax.axis_size("head")
    rows, width = packed.shape
    moved = lax.all_to_all(packed, "head", split_axis=0, concat_axis=1, tiled=True)
    moved = moved.reshape(rows // count, count, 2, width // 2)
    return [moved[:, :, i].reshape(rows // count, count * width // 2) for i in range(2)]


def from_behind(value, axis, steps):
    count = lax.axis_size(axis)
    pairs = [(source, (source + steps) % count) for source in range(count)]
    return lax.ppermute(value, axis, pairs)


def attention_kernel(
    picks_ref, qd_ref, kv_ref, left_ref, right_ref,
    out_ref, highest_ref, inverse_ref, delta_ref, to_left_ref, to_right_ref, left_acc, right_acc,
):
    number = pl.program_id(0)
    scale = HEAD_DIM ** (-0.5)
    f32 = jnp.float32

    @pl.when(number == 0)
    def _():
        left_acc[...] = jnp.zeros(left_acc.shape, f32)
        right_acc[...] = jnp.zeros(right_acc.shape, f32)

    packed = qd_ref[0]
    lane = lax.broadcasted_iota(jnp.int32, packed.shape, 1)
    low = lane < HEAD_DIM
    zero = jnp.zeros_like(packed)
    query_ext = jnp.where(low, packed, zero)
    grad_ext = jnp.where(low, zero, packed)
    pairs = (kv_ref[0], left_ref[0], right_ref[0])

    def nt(a, b):
        return lax.dot_general(a, b, (((1,), (1,)), ((), ())), preferred_element_type=f32)

    def nn(a, b):
        return lax.dot_general(a, b, (((1,), (0,)), ((), ())), preferred_element_type=f32)

    def tn(a, b):
        return lax.dot_general(a, b, (((0,), (0,)), ((), ())), preferred_element_type=f32)

    scores = [nt(query_ext, pair) * scale for pair in pairs]
    row = lax.broadcasted_iota(jnp.int32, scores[0].shape, 0)
    col = lax.broadcasted_iota(jnp.int32, scores[0].shape, 1)
    scores[0] = jnp.where(col <= row, scores[0], -jnp.inf)
    highest = jnp.max(scores[0], axis=1, keepdims=True)
    for part in scores[1:]:
        highest = jnp.maximum(highest, jnp.max(part, axis=1, keepdims=True))
    shifted = [jnp.exp(part - highest) for part in scores]
    total = sum(jnp.sum(part, axis=1, keepdims=True) for part in shifted)
    inverse = 1.0 / total
    weights = [part * inverse for part in shifted]
    weights_bf = [w.astype(jnp.bfloat16) for w in weights]
    attended = sum(nn(w, pair) for w, pair in zip(weights_bf, pairs)).astype(jnp.bfloat16)
    products = jnp.where(low, 0.0, packed.astype(f32) * attended.astype(f32))
    row_delta = jnp.sum(products, axis=1, keepdims=True)
    score_grads = [
        (w * (nt(grad_ext, pair) - row_delta)).astype(jnp.bfloat16) for w, pair in zip(weights, pairs)
    ]
    query_grad = (sum(nn(d, pair) for d, pair in zip(score_grads, pairs)) * scale).astype(jnp.bfloat16)
    out_rows = jnp.where(low, query_grad.astype(f32), attended.astype(f32))
    chunk = out_ref.shape[1]
    for j in range(out_ref.shape[0]):
        out_ref[j] = jnp.transpose(out_rows[j * chunk : (j + 1) * chunk]).astype(jnp.bfloat16)
    highest_ref[0] = highest
    inverse_ref[0] = inverse
    delta_ref[0] = row_delta
    kv_parts = [None] + [
        jnp.where(low, tn(d, packed) * scale, tn(w, packed))
        for d, w in zip(score_grads[1:], weights_bf[1:])
    ]
    left_pick = picks_ref[0, number]
    right_pick = picks_ref[1, number]
    left_acc[left_pick] += kv_parts[1]
    right_acc[right_pick] += kv_parts[2]

    @pl.when(number == pl.num_programs(0) - 1)
    def _():
        to_left_ref[...] = left_acc[...].astype(jnp.bfloat16)
        to_right_ref[...] = right_acc[...].astype(jnp.bfloat16)


def own_kernel(qd_ref, kv_ref, highest_ref, inverse_ref, delta_ref, own_grad_ref):
    scale = HEAD_DIM ** (-0.5)
    f32 = jnp.float32
    packed = qd_ref[0]
    pair = kv_ref[0]
    lane = lax.broadcasted_iota(jnp.int32, packed.shape, 1)
    low = lane < HEAD_DIM
    zero = jnp.zeros_like(packed)
    query_ext = jnp.where(low, packed, zero)
    grad_ext = jnp.where(low, zero, packed)
    score = lax.dot_general(query_ext, pair, (((1,), (1,)), ((), ())), preferred_element_type=f32) * scale
    row = lax.broadcasted_iota(jnp.int32, score.shape, 0)
    col = lax.broadcasted_iota(jnp.int32, score.shape, 1)
    score = jnp.where(col <= row, score, -jnp.inf)
    weight = jnp.exp(score - highest_ref[0]) * inverse_ref[0]
    weight_grad = lax.dot_general(grad_ext, pair, (((1,), (1,)), ((), ())), preferred_element_type=f32)
    score_grad = (weight * (weight_grad - delta_ref[0])).astype(jnp.bfloat16)
    key_part = lax.dot_general(score_grad, packed, (((0,), (0,)), ((), ())), preferred_element_type=f32)
    value_part = lax.dot_general(
        weight.astype(jnp.bfloat16), packed, (((0,), (0,)), ((), ())), preferred_element_type=f32
    )
    own_grad_ref[0] = jnp.where(low, key_part * scale, value_part)


def own_grads_of(qd, kv, highest, inverse, delta):
    block_count, block, width = kv.shape
    one_spec = pl.BlockSpec((1, block, width), lambda n: (n, 0, 0))
    stat_spec = pl.BlockSpec((1, block, 1), lambda n: (n, 0, 0))
    return pl.pallas_call(
        own_kernel,
        grid=(block_count,),
        in_specs=[one_spec, one_spec, stat_spec, stat_spec, stat_spec],
        out_specs=one_spec,
        out_shape=jax.ShapeDtypeStruct((block_count, block, width), jnp.float32),
        compiler_params=pltpu.CompilerParams(dimension_semantics=("arbitrary",)),
        interpret=INTERPRET,
    )(qd, kv, highest, inverse, delta)


def attention(picks, qd, kv, left, right):
    block_count, block, width = kv.shape
    left_spec = pl.BlockSpec((1, block, width), lambda n, p: (p[0, n], 0, 0))
    right_spec = pl.BlockSpec((1, block, width), lambda n, p: (p[1, n], 0, 0))
    one_spec = pl.BlockSpec((1, block, width), lambda n, p: (n, 0, 0))
    whole_spec = pl.BlockSpec((block_count, block, width), lambda n, p: (0, 0, 0))
    stat_spec = pl.BlockSpec((1, block, 1), lambda n, p: (n, 0, 0))
    chunks = block // width
    chunk_spec = pl.BlockSpec((chunks, width, width), lambda n, p: (n, 0, 0))
    shape = (block_count, block, width)
    stat = jax.ShapeDtypeStruct((block_count, block, 1), jnp.float32)
    return pl.pallas_call(
        attention_kernel,
        grid_spec=pltpu.PrefetchScalarGridSpec(
            num_scalar_prefetch=1,
            grid=(block_count,),
            in_specs=[one_spec, one_spec, left_spec, right_spec],
            out_specs=[chunk_spec, stat_spec, stat_spec, stat_spec, whole_spec, whole_spec],
            scratch_shapes=[pltpu.VMEM(shape, jnp.float32), pltpu.VMEM(shape, jnp.float32)],
        ),
        out_shape=[
            jax.ShapeDtypeStruct((block_count * chunks, width, width), jnp.bfloat16),
            stat,
            stat,
            stat,
            jax.ShapeDtypeStruct(shape, jnp.bfloat16),
            jax.ShapeDtypeStruct(shape, jnp.bfloat16),
        ],
        compiler_params=pltpu.CompilerParams(dimension_semantics=("arbitrary",)),
        interpret=INTERPRET,
    )(picks, qd, kv, left, right)


def shards(query_rows, key_rows, value_rows, out_grad, neighbour_blocks):
    kv_heads = to_heads(key_rows, value_rows)
    row_count, width = kv_heads.shape
    block_count = row_count // BLOCK
    kv = kv_heads.reshape(block_count, BLOCK, width)
    count = lax.axis_size("blk")
    near_pairs = [(i, i ^ 1) for i in range(count)]
    far_pairs = [(i, (i + 1 if i % 2 else i - 1) % count) for i in range(count)]
    near = lax.ppermute(kv, "blk", near_pairs)
    far = lax.ppermute(kv, "blk", far_pairs)
    qd = to_heads(query_rows, out_grad).reshape(block_count, BLOCK, width)
    place = lax.axis_index("blk")
    first_row = place * block_count
    picks = [lax.dynamic_slice_in_dim(neighbour_blocks[:, c], first_row, block_count, 0) for c in range(2)]
    even = place % 2 == 0
    picks = jnp.stack([jnp.where(even, picks[1], picks[0]), jnp.where(even, picks[0], picks[1])])
    picks = jnp.clip(picks, 0, block_count - 1).astype(jnp.int32)
    out_pair, highest, inverse, delta, to_near, to_far = attention(picks, qd, kv, near, far)
    from_near = lax.ppermute(to_near, "blk", near_pairs).astype(jnp.float32)
    from_far = lax.ppermute(to_far, "blk", far_pairs).astype(jnp.float32)
    own_grads = own_grads_of(qd, kv, highest, inverse, delta)
    query_grad, attended = to_rows(out_pair.transpose(0, 2, 1).reshape(row_count, width))
    kv_grads = (own_grads + from_near + from_far).astype(jnp.bfloat16)
    key_grad, value_grad = to_rows(kv_grads.reshape(row_count, width))
    return (attended, query_grad, key_grad, value_grad)


def solution(mesh):
    in_specs = (
        P(("blk", "head"), None),
        P(("blk", "head"), None),
        P(("blk", "head"), None),
        P(("blk", "head"), None),
        P(),
    )
    out_specs = (
        P(("blk", "head"), None),
        P(("blk", "head"), None),
        P(("blk", "head"), None),
        P(("blk", "head"), None),
    )
    return jax.shard_map(shards, mesh=mesh, in_specs=in_specs, out_specs=out_specs, check_vma=False)
```

```python
import jax
import jax.numpy as jnp
from jax import lax
from jax.experimental import pallas as pl
from jax.experimental.pallas import tpu as pltpu
from jax.sharding import PartitionSpec as P

HEAD_DIM = 64
BLOCK = 512
INTERPRET = False


def to_heads(first, second):
    count = lax.axis_size("head")
    rows, width = first.shape
    split = [a.reshape(rows, count, width // count) for a in (first, second)]
    packed = jnp.concatenate(split, axis=2)
    moved = lax.all_to_all(packed, "head", split_axis=1, concat_axis=0, tiled=True)
    return moved.reshape(count * rows, 2 * width // count)


def to_rows(packed):
    count = lax.axis_size("head")
    rows, width = packed.shape
    moved = lax.all_to_all(packed, "head", split_axis=0, concat_axis=1, tiled=True)
    moved = moved.reshape(rows // count, count, 2, width // 2)
    return [moved[:, :, i].reshape(rows // count, count * width // 2) for i in range(2)]


def from_behind(value, axis, steps):
    count = lax.axis_size(axis)
    pairs = [(source, (source + steps) % count) for source in range(count)]
    return lax.ppermute(value, axis, pairs)


def attention_kernel(
    picks_ref, qd_ref, kv_ref, left_ref, right_ref,
    out_ref, highest_ref, inverse_ref, delta_ref, to_left_ref, to_right_ref, left_acc, right_acc,
):
    number = pl.program_id(0)
    scale = HEAD_DIM ** (-0.5)
    f32 = jnp.float32

    @pl.when(number == 0)
    def _():
        left_acc[...] = jnp.zeros(left_acc.shape, f32)
        right_acc[...] = jnp.zeros(right_acc.shape, f32)

    packed = qd_ref[0]
    lane = lax.broadcasted_iota(jnp.int32, packed.shape, 1)
    low = lane < HEAD_DIM
    zero = jnp.zeros_like(packed)
    query_ext = jnp.where(low, packed, zero)
    grad_ext = jnp.where(low, zero, packed)
    pairs = (kv_ref[0], left_ref[0], right_ref[0])

    def nt(a, b):
        return lax.dot_general(a, b, (((1,), (1,)), ((), ())), preferred_element_type=f32)

    def nn(a, b):
        return lax.dot_general(a, b, (((1,), (0,)), ((), ())), preferred_element_type=f32)

    def tn(a, b):
        return lax.dot_general(a, b, (((0,), (0,)), ((), ())), preferred_element_type=f32)

    scores = [nt(query_ext, pair) * scale for pair in pairs]
    row = lax.broadcasted_iota(jnp.int32, scores[0].shape, 0)
    col = lax.broadcasted_iota(jnp.int32, scores[0].shape, 1)
    scores[0] = jnp.where(col <= row, scores[0], -jnp.inf)
    highest = jnp.max(scores[0], axis=1, keepdims=True)
    for part in scores[1:]:
        highest = jnp.maximum(highest, jnp.max(part, axis=1, keepdims=True))
    shifted = [jnp.exp(part - highest) for part in scores]
    total = sum(jnp.sum(part, axis=1, keepdims=True) for part in shifted)
    inverse = 1.0 / total
    weights = [part * inverse for part in shifted]
    weights_bf = [w.astype(jnp.bfloat16) for w in weights]
    attended = sum(nn(w, pair) for w, pair in zip(weights_bf, pairs)).astype(jnp.bfloat16)
    products = jnp.where(low, 0.0, packed.astype(f32) * attended.astype(f32))
    row_delta = jnp.sum(products, axis=1, keepdims=True)
    score_grads = [
        (w * (nt(grad_ext, pair) - row_delta)).astype(jnp.bfloat16) for w, pair in zip(weights, pairs)
    ]
    query_grad = (sum(nn(d, pair) for d, pair in zip(score_grads, pairs)) * scale).astype(jnp.bfloat16)
    out_rows = jnp.where(low, query_grad.astype(f32), attended.astype(f32))
    chunk = out_ref.shape[1]
    for j in range(out_ref.shape[0]):
        out_ref[j] = jnp.transpose(out_rows[j * chunk : (j + 1) * chunk]).astype(jnp.bfloat16)
    highest_ref[0] = highest
    inverse_ref[0] = inverse
    delta_ref[0] = row_delta
    kv_parts = [None] + [
        jnp.where(low, tn(d, packed) * scale, tn(w, packed))
        for d, w in zip(score_grads[1:], weights_bf[1:])
    ]
    left_pick = picks_ref[0, number]
    right_pick = picks_ref[1, number]
    left_acc[left_pick] += kv_parts[1]
    right_acc[right_pick] += kv_parts[2]

    @pl.when(number == pl.num_programs(0) - 1)
    def _():
        to_left_ref[...] = left_acc[...].astype(jnp.bfloat16)
        to_right_ref[...] = right_acc[...].astype(jnp.bfloat16)


def own_kernel(qd_ref, kv_ref, highest_ref, inverse_ref, delta_ref, own_grad_ref):
    scale = HEAD_DIM ** (-0.5)
    f32 = jnp.float32
    packed = qd_ref[0]
    pair = kv_ref[0]
    lane = lax.broadcasted_iota(jnp.int32, packed.shape, 1)
    low = lane < HEAD_DIM
    zero = jnp.zeros_like(packed)
    query_ext = jnp.where(low, packed, zero)
    grad_ext = jnp.where(low, zero, packed)
    score = lax.dot_general(query_ext, pair, (((1,), (1,)), ((), ())), preferred_element_type=f32) * scale
    row = lax.broadcasted_iota(jnp.int32, score.shape, 0)
    col = lax.broadcasted_iota(jnp.int32, score.shape, 1)
    score = jnp.where(col <= row, score, -jnp.inf)
    weight = jnp.exp(score - highest_ref[0]) * inverse_ref[0]
    weight_grad = lax.dot_general(grad_ext, pair, (((1,), (1,)), ((), ())), preferred_element_type=f32)
    score_grad = (weight * (weight_grad - delta_ref[0])).astype(jnp.bfloat16)
    key_part = lax.dot_general(score_grad, packed, (((0,), (0,)), ((), ())), preferred_element_type=f32)
    value_part = lax.dot_general(
        weight.astype(jnp.bfloat16), packed, (((0,), (0,)), ((), ())), preferred_element_type=f32
    )
    own_grad_ref[0] = jnp.where(low, key_part * scale, value_part)


def own_grads_of(qd, kv, highest, inverse, delta):
    block_count, block, width = kv.shape
    one_spec = pl.BlockSpec((1, block, width), lambda n: (n, 0, 0))
    stat_spec = pl.BlockSpec((1, block, 1), lambda n: (n, 0, 0))
    return pl.pallas_call(
        own_kernel,
        grid=(block_count,),
        in_specs=[one_spec, one_spec, stat_spec, stat_spec, stat_spec],
        out_specs=one_spec,
        out_shape=jax.ShapeDtypeStruct((block_count, block, width), jnp.float32),
        compiler_params=pltpu.CompilerParams(dimension_semantics=("arbitrary",)),
        interpret=INTERPRET,
    )(qd, kv, highest, inverse, delta)


def sum_kernel(own_ref, near_ref, far_ref, out_ref):
    total = own_ref[0] + near_ref[0].astype(jnp.float32) + far_ref[0].astype(jnp.float32)
    chunk = out_ref.shape[1]
    for j in range(out_ref.shape[0]):
        out_ref[j] = jnp.transpose(total[j * chunk : (j + 1) * chunk]).astype(jnp.bfloat16)


def summed(own, near, far):
    block_count, block, width = own.shape
    chunks = block // width
    one_spec = pl.BlockSpec((1, block, width), lambda n: (n, 0, 0))
    return pl.pallas_call(
        sum_kernel,
        grid=(block_count,),
        in_specs=[one_spec, one_spec, one_spec],
        out_specs=pl.BlockSpec((chunks, width, width), lambda n: (n, 0, 0)),
        out_shape=jax.ShapeDtypeStruct((block_count * chunks, width, width), jnp.bfloat16),
        compiler_params=pltpu.CompilerParams(dimension_semantics=("arbitrary",)),
        interpret=INTERPRET,
    )(own, near, far)


def attention(picks, qd, kv, left, right):
    block_count, block, width = kv.shape
    left_spec = pl.BlockSpec((1, block, width), lambda n, p: (p[0, n], 0, 0))
    right_spec = pl.BlockSpec((1, block, width), lambda n, p: (p[1, n], 0, 0))
    one_spec = pl.BlockSpec((1, block, width), lambda n, p: (n, 0, 0))
    whole_spec = pl.BlockSpec((block_count, block, width), lambda n, p: (0, 0, 0))
    stat_spec = pl.BlockSpec((1, block, 1), lambda n, p: (n, 0, 0))
    chunks = block // width
    chunk_spec = pl.BlockSpec((chunks, width, width), lambda n, p: (n, 0, 0))
    shape = (block_count, block, width)
    stat = jax.ShapeDtypeStruct((block_count, block, 1), jnp.float32)
    return pl.pallas_call(
        attention_kernel,
        grid_spec=pltpu.PrefetchScalarGridSpec(
            num_scalar_prefetch=1,
            grid=(block_count,),
            in_specs=[one_spec, one_spec, left_spec, right_spec],
            out_specs=[chunk_spec, stat_spec, stat_spec, stat_spec, whole_spec, whole_spec],
            scratch_shapes=[pltpu.VMEM(shape, jnp.float32), pltpu.VMEM(shape, jnp.float32)],
        ),
        out_shape=[
            jax.ShapeDtypeStruct((block_count * chunks, width, width), jnp.bfloat16),
            stat,
            stat,
            stat,
            jax.ShapeDtypeStruct(shape, jnp.bfloat16),
            jax.ShapeDtypeStruct(shape, jnp.bfloat16),
        ],
        compiler_params=pltpu.CompilerParams(dimension_semantics=("arbitrary",)),
        interpret=INTERPRET,
    )(picks, qd, kv, left, right)


def shards(query_rows, key_rows, value_rows, out_grad, neighbour_blocks):
    kv_heads = to_heads(key_rows, value_rows)
    row_count, width = kv_heads.shape
    block_count = row_count // BLOCK
    kv = kv_heads.reshape(block_count, BLOCK, width)
    count = lax.axis_size("blk")
    near_pairs = [(i, i ^ 1) for i in range(count)]
    far_pairs = [(i, (i + 1 if i % 2 else i - 1) % count) for i in range(count)]
    near = lax.ppermute(kv, "blk", near_pairs)
    far = lax.ppermute(kv, "blk", far_pairs)
    qd = to_heads(query_rows, out_grad).reshape(block_count, BLOCK, width)
    place = lax.axis_index("blk")
    first_row = place * block_count
    picks = [lax.dynamic_slice_in_dim(neighbour_blocks[:, c], first_row, block_count, 0) for c in range(2)]
    even = place % 2 == 0
    picks = jnp.stack([jnp.where(even, picks[1], picks[0]), jnp.where(even, picks[0], picks[1])])
    picks = jnp.clip(picks, 0, block_count - 1).astype(jnp.int32)
    out_pair, highest, inverse, delta, to_near, to_far = attention(picks, qd, kv, near, far)
    from_near = lax.ppermute(to_near, "blk", near_pairs)
    from_far = lax.ppermute(to_far, "blk", far_pairs)
    own_grads = own_grads_of(qd, kv, highest, inverse, delta)
    query_grad, attended = to_rows(out_pair.transpose(0, 2, 1).reshape(row_count, width))
    kv_grads = summed(own_grads, from_near, from_far)
    key_grad, value_grad = to_rows(kv_grads.transpose(0, 2, 1).reshape(row_count, width))
    return (attended, query_grad, key_grad, value_grad)


def solution(mesh):
    in_specs = (
        P(("blk", "head"), None),
        P(("blk", "head"), None),
        P(("blk", "head"), None),
        P(("blk", "head"), None),
        P(),
    )
    out_specs = (
        P(("blk", "head"), None),
        P(("blk", "head"), None),
        P(("blk", "head"), None),
        P(("blk", "head"), None),
    )
    return jax.shard_map(shards, mesh=mesh, in_specs=in_specs, out_specs=out_specs, check_vma=False)
```

```python
import jax
import jax.numpy as jnp
from jax import lax
from jax.experimental import pallas as pl
from jax.experimental.pallas import tpu as pltpu
from jax.sharding import PartitionSpec as P

HEAD_DIM = 64
BLOCK = 512
INTERPRET = False


def to_heads(first, second):
    count = lax.axis_size("head")
    rows, width = first.shape
    split = [a.reshape(rows, count, width // count) for a in (first, second)]
    packed = jnp.concatenate(split, axis=2)
    moved = lax.all_to_all(packed, "head", split_axis=1, concat_axis=0, tiled=True)
    return moved.reshape(count * rows, 2 * width // count)


def to_rows(packed):
    count = lax.axis_size("head")
    rows, width = packed.shape
    moved = lax.all_to_all(packed, "head", split_axis=0, concat_axis=1, tiled=True)
    moved = moved.reshape(rows // count, count, 2, width // 2)
    return [moved[:, :, i].reshape(rows // count, count * width // 2) for i in range(2)]


def from_behind(value, axis, steps):
    count = lax.axis_size(axis)
    pairs = [(source, (source + steps) % count) for source in range(count)]
    return lax.ppermute(value, axis, pairs)


def attention_kernel(
    picks_ref, qd_ref, kv_ref, left_ref, right_ref,
    out_ref, stats_ref, to_left_ref, to_right_ref, left_acc, right_acc,
):
    number = pl.program_id(0)
    scale = HEAD_DIM ** (-0.5)
    f32 = jnp.float32

    @pl.when(number == 0)
    def _():
        left_acc[...] = jnp.zeros(left_acc.shape, f32)
        right_acc[...] = jnp.zeros(right_acc.shape, f32)

    packed = qd_ref[0]
    lane = lax.broadcasted_iota(jnp.int32, packed.shape, 1)
    low = lane < HEAD_DIM
    zero = jnp.zeros_like(packed)
    query_ext = jnp.where(low, packed, zero)
    grad_ext = jnp.where(low, zero, packed)
    pairs = (kv_ref[0], left_ref[0], right_ref[0])

    def nt(a, b):
        return lax.dot_general(a, b, (((1,), (1,)), ((), ())), preferred_element_type=f32)

    def nn(a, b):
        return lax.dot_general(a, b, (((1,), (0,)), ((), ())), preferred_element_type=f32)

    def tn(a, b):
        return lax.dot_general(a, b, (((0,), (0,)), ((), ())), preferred_element_type=f32)

    scores = [nt(query_ext, pair) * scale for pair in pairs]
    row = lax.broadcasted_iota(jnp.int32, scores[0].shape, 0)
    col = lax.broadcasted_iota(jnp.int32, scores[0].shape, 1)
    scores[0] = jnp.where(col <= row, scores[0], -jnp.inf)
    highest = jnp.max(scores[0], axis=1, keepdims=True)
    for part in scores[1:]:
        highest = jnp.maximum(highest, jnp.max(part, axis=1, keepdims=True))
    shifted = [jnp.exp(part - highest) for part in scores]
    total = sum(jnp.sum(part, axis=1, keepdims=True) for part in shifted)
    inverse = 1.0 / total
    weights = [part * inverse for part in shifted]
    weights_bf = [w.astype(jnp.bfloat16) for w in weights]
    attended = sum(nn(w, pair) for w, pair in zip(weights_bf, pairs)).astype(jnp.bfloat16)
    products = jnp.where(low, 0.0, packed.astype(f32) * attended.astype(f32))
    row_delta = jnp.sum(products, axis=1, keepdims=True)
    score_grads = [
        (w * (nt(grad_ext, pair) - row_delta)).astype(jnp.bfloat16) for w, pair in zip(weights, pairs)
    ]
    query_grad = (sum(nn(d, pair) for d, pair in zip(score_grads, pairs)) * scale).astype(jnp.bfloat16)
    out_rows = jnp.where(low, query_grad.astype(f32), attended.astype(f32))
    chunk = out_ref.shape[1]
    for j in range(out_ref.shape[0]):
        out_ref[j] = jnp.transpose(out_rows[j * chunk : (j + 1) * chunk]).astype(jnp.bfloat16)
    stats_ref[0] = jnp.where(lane == 0, highest, jnp.where(lane == 1, inverse, row_delta))
    kv_parts = [None] + [
        jnp.where(low, tn(d, packed) * scale, tn(w, packed))
        for d, w in zip(score_grads[1:], weights_bf[1:])
    ]
    left_pick = picks_ref[0, number]
    right_pick = picks_ref[1, number]
    left_acc[left_pick] += kv_parts[1]
    right_acc[right_pick] += kv_parts[2]

    @pl.when(number == pl.num_programs(0) - 1)
    def _():
        to_left_ref[...] = left_acc[...].astype(jnp.bfloat16)
        to_right_ref[...] = right_acc[...].astype(jnp.bfloat16)


def own_kernel(qd_ref, kv_ref, stats_ref, own_grad_ref):
    scale = HEAD_DIM ** (-0.5)
    f32 = jnp.float32
    packed = qd_ref[0]
    pair = kv_ref[0]
    lane = lax.broadcasted_iota(jnp.int32, packed.shape, 1)
    low = lane < HEAD_DIM
    zero = jnp.zeros_like(packed)
    query_ext = jnp.where(low, packed, zero)
    grad_ext = jnp.where(low, zero, packed)
    score = lax.dot_general(query_ext, pair, (((1,), (1,)), ((), ())), preferred_element_type=f32) * scale
    row = lax.broadcasted_iota(jnp.int32, score.shape, 0)
    col = lax.broadcasted_iota(jnp.int32, score.shape, 1)
    score = jnp.where(col <= row, score, -jnp.inf)
    stats = stats_ref[0]
    weight = jnp.exp(score - stats[:, 0:1]) * stats[:, 1:2]
    weight_grad = lax.dot_general(grad_ext, pair, (((1,), (1,)), ((), ())), preferred_element_type=f32)
    score_grad = (weight * (weight_grad - stats[:, 2:3])).astype(jnp.bfloat16)
    key_part = lax.dot_general(score_grad, packed, (((0,), (0,)), ((), ())), preferred_element_type=f32)
    value_part = lax.dot_general(
        weight.astype(jnp.bfloat16), packed, (((0,), (0,)), ((), ())), preferred_element_type=f32
    )
    own_grad_ref[0] = jnp.where(low, key_part * scale, value_part)


def own_grads_of(qd, kv, stats):
    block_count, block, width = kv.shape
    one_spec = pl.BlockSpec((1, block, width), lambda n: (n, 0, 0))
    return pl.pallas_call(
        own_kernel,
        grid=(block_count,),
        in_specs=[one_spec, one_spec, one_spec],
        out_specs=one_spec,
        out_shape=jax.ShapeDtypeStruct((block_count, block, width), jnp.float32),
        compiler_params=pltpu.CompilerParams(dimension_semantics=("arbitrary",)),
        interpret=INTERPRET,
    )(qd, kv, stats)


def attention(picks, qd, kv, left, right):
    block_count, block, width = kv.shape
    left_spec = pl.BlockSpec((1, block, width), lambda n, p: (p[0, n], 0, 0))
    right_spec = pl.BlockSpec((1, block, width), lambda n, p: (p[1, n], 0, 0))
    one_spec = pl.BlockSpec((1, block, width), lambda n, p: (n, 0, 0))
    whole_spec = pl.BlockSpec((block_count, block, width), lambda n, p: (0, 0, 0))
    chunks = block // width
    chunk_spec = pl.BlockSpec((chunks, width, width), lambda n, p: (n, 0, 0))
    shape = (block_count, block, width)
    return pl.pallas_call(
        attention_kernel,
        grid_spec=pltpu.PrefetchScalarGridSpec(
            num_scalar_prefetch=1,
            grid=(block_count,),
            in_specs=[one_spec, one_spec, left_spec, right_spec],
            out_specs=[chunk_spec, one_spec, whole_spec, whole_spec],
            scratch_shapes=[pltpu.VMEM(shape, jnp.float32), pltpu.VMEM(shape, jnp.float32)],
        ),
        out_shape=[
            jax.ShapeDtypeStruct((block_count * chunks, width, width), jnp.bfloat16),
            jax.ShapeDtypeStruct(shape, jnp.float32),
            jax.ShapeDtypeStruct(shape, jnp.bfloat16),
            jax.ShapeDtypeStruct(shape, jnp.bfloat16),
        ],
        compiler_params=pltpu.CompilerParams(dimension_semantics=("arbitrary",)),
        interpret=INTERPRET,
    )(picks, qd, kv, left, right)


def shards(query_rows, key_rows, value_rows, out_grad, neighbour_blocks):
    kv_heads = to_heads(key_rows, value_rows)
    row_count, width = kv_heads.shape
    block_count = row_count // BLOCK
    kv = kv_heads.reshape(block_count, BLOCK, width)
    count = lax.axis_size("blk")
    near_pairs = [(i, i ^ 1) for i in range(count)]
    far_pairs = [(i, (i + 1 if i % 2 else i - 1) % count) for i in range(count)]
    near = lax.ppermute(kv, "blk", near_pairs)
    far = lax.ppermute(kv, "blk", far_pairs)
    qd = to_heads(query_rows, out_grad).reshape(block_count, BLOCK, width)
    place = lax.axis_index("blk")
    first_row = place * block_count
    picks = [lax.dynamic_slice_in_dim(neighbour_blocks[:, c], first_row, block_count, 0) for c in range(2)]
    even = place % 2 == 0
    picks = jnp.stack([jnp.where(even, picks[1], picks[0]), jnp.where(even, picks[0], picks[1])])
    picks = jnp.clip(picks, 0, block_count - 1).astype(jnp.int32)
    out_pair, stats, to_near, to_far = attention(picks, qd, kv, near, far)
    from_near = lax.ppermute(to_near, "blk", near_pairs).astype(jnp.float32)
    from_far = lax.ppermute(to_far, "blk", far_pairs).astype(jnp.float32)
    own_grads = own_grads_of(qd, kv, stats)
    query_grad, attended = to_rows(out_pair.transpose(0, 2, 1).reshape(row_count, width))
    kv_grads = (own_grads + from_near + from_far).astype(jnp.bfloat16)
    key_grad, value_grad = to_rows(kv_grads.reshape(row_count, width))
    return (attended, query_grad, key_grad, value_grad)


def solution(mesh):
    in_specs = (
        P(("blk", "head"), None),
        P(("blk", "head"), None),
        P(("blk", "head"), None),
        P(("blk", "head"), None),
        P(),
    )
    out_specs = (
        P(("blk", "head"), None),
        P(("blk", "head"), None),
        P(("blk", "head"), None),
        P(("blk", "head"), None),
    )
    return jax.shard_map(shards, mesh=mesh, in_specs=in_specs, out_specs=out_specs, check_vma=False)
```
